768 devices in a mesh: gx: 64 (over y, x, core), gy: 12 (over z).
Axes of the slice: x: 4, y: 8, z: 12, core: 2. Of those that a mesh axis runs over, the one named last changes fastest.
Arguments:
- rhs_field: float32 [3, 128, 384, 128], P(None, 'gx', 'gy'), may hold values from -6 to 6
- shear_modulus: float32 [128, 384, 128], P('gx', 'gy'), may hold values from 0.3 to 3
- lame_lambda: float32 [128, 384, 128], P('gx', 'gy'), may hold values from 0.3 to 3
- group_start: int32 [64, 12], P('gx'), may hold values from 0 to 1, as said below
Outputs:
- solution_field: float32 [3, 128, 384, 128], P(None, 'gx', 'gy')
- residual_field: float32 [3, 128, 384, 128], P(None, 'gx', 'gy')
The draws below stay inside these ranges and needn't reach their ends.
Inputs may be any that keep to these rules, and one draw needn't show every extreme that they name: `group_start`: each index of gx has exactly one 1, at an index of gy from 1 to 11.
All inputs are finite; a program needn't handle non-finite values.
Results may differ from the reference program's by a relative error of at most 0.00011.
Values sent between devices are 32-bit elements; how exact they have to be, the bound alone decides.
No kernel may reach another device: no remote copies, remote signals or barrier semaphores. Data moves between devices by JAX's collectives and lax.ppermute only.
A program may use at most 32 MiB of HBM per device.

```python
import math
import jax
import jax.numpy as jnp

CX = 2
CY = 32
SWEEPS = 3
COARSE_SWEEPS = 4
NX = 128
NY = 384
NZ = 128
N_GX = 64
N_GY = 12


def draw_rhs_field(key, part):
    full_shape = (3, NX, NY, NZ)
    return jnp.clip(jax.random.normal(key, full_shape, jnp.float32) + 1.0, -6.0, 6.0)


def draw_group_start(key, part):
    split_at = jax.random.randint(jax.random.fold_in(key, 7), (N_GX, 1), 1, N_GY)
    return jnp.where(jnp.arange(N_GY, dtype=jnp.int32)[None, :] == split_at, 1, 0).astype(jnp.int32)


def block_levels(stream_key, shape, shards, low, high):
    loudness, own = 1.0, jax.random.fold_in(stream_key, 6)
    for position, parts in shards:
        heights = jnp.exp(jax.random.uniform(jax.random.fold_in(own, position), (parts,), jnp.float32, low / len(shards), high / len(shards)))
        loudness = loudness * jnp.repeat(heights, shape[position] // parts).reshape([-1 if axis == position else 1 for axis in range(len(shape))])
    return loudness


def setup_inputs(seed: int = 0) -> dict:
    arg_keys = jax.random.split(jax.random.key(seed), 5)
    rhs_field = draw_rhs_field(jax.random.fold_in(arg_keys[4], 71), 0)
    shear_modulus = jnp.clip(jnp.exp(math.log(3.0) - 2.3025851 * jax.random.uniform(arg_keys[1], (NX, NY, NZ), jnp.float32) ** block_levels(arg_keys[1], (NX, NY, NZ), ((0, 64), (1, 12)), -0.2, 0.2)), 0.3, 3.0)
    lame_lambda = jnp.clip(jnp.exp(math.log(3.0) - 2.3025851 * jax.random.uniform(arg_keys[2], (NX, NY, NZ), jnp.float32) ** block_levels(arg_keys[2], (NX, NY, NZ), ((0, 64), (1, 12)), -0.2, 0.2)), 0.3, 3.0)
    group_start = draw_group_start(jax.random.fold_in(arg_keys[4], 71), 0)
    return dict(rhs_field=rhs_field, shear_modulus=shear_modulus, lame_lambda=lame_lambda, group_start=group_start)


LOW_BOUND = 0.5
HIGH_BOUND = 6.0
SHIFT_SCALE = 48.0
UNITS = ((1, 0, 0), (0, 1, 0), (0, 0, 1))


def shifted(array, step_x, step_y, step_z):
    size_x = array.shape[-3] - 2
    size_y = array.shape[-2] - 2
    size_z = array.shape[-1] - 2
    return array[..., 1 + step_x:1 + step_x + size_x, 1 + step_y:1 + step_y + size_y, 1 + step_z:1 + step_z + size_z]


def diagonal(mu_pad, lam_pad, scale):
    mu_centre = shifted(mu_pad, 0, 0, 0)
    lam_centre = shifted(lam_pad, 0, 0, 0)
    faces = 0.0
    for unit in UNITS:
        backward = tuple(-value for value in unit)
        faces = faces + 0.5 * (mu_centre + shifted(mu_pad, *unit)) + 0.5 * (mu_centre + shifted(mu_pad, *backward))
    results = []
    for unit in UNITS:
        backward = tuple(-value for value in unit)
        results.append(scale * (faces + lam_centre + shifted(lam_pad, *backward)))
    return jnp.stack(results)


def operate(field_pad, mu_pad, lam_pad, scale):
    mu_centre = shifted(mu_pad, 0, 0, 0)
    lam_centre = shifted(lam_pad, 0, 0, 0)
    components = [field_pad[0], field_pad[1], field_pad[2]]
    centres = [shifted(value, 0, 0, 0) for value in components]
    laplace = [0.0, 0.0, 0.0]
    for unit in UNITS:
        backward = tuple(-value for value in unit)
        face_up = 0.5 * (mu_centre + shifted(mu_pad, *unit))
        face_down = 0.5 * (mu_centre + shifted(mu_pad, *backward))
        for comp_id in range(3):
            laplace[comp_id] = laplace[comp_id] + face_up * (shifted(components[comp_id], *unit) - centres[comp_id]) - face_down * (centres[comp_id] - shifted(components[comp_id], *backward))

    def spread(offset):
        total = 0.0
        for comp_id in range(3):
            ahead = tuple(offset[axis_id] + UNITS[comp_id][axis_id] for axis_id in range(3))
            total = total + (shifted(components[comp_id], *ahead) - shifted(components[comp_id], *offset))
        return total

    stress_here = lam_centre * spread((0, 0, 0))
    results = []
    for comp_id in range(3):
        backward = tuple(-value for value in UNITS[comp_id])
        grad_term = stress_here - shifted(lam_pad, *backward) * spread(backward)
        results.append(scale * (-laplace[comp_id] - grad_term))
    return jnp.stack(results)


def smooth(solution, residual, inverse_diag, apply_fn, steps):
    midpoint = 0.5 * (HIGH_BOUND + LOW_BOUND)
    halfwidth = 0.5 * (HIGH_BOUND - LOW_BOUND)
    sharpness = midpoint / halfwidth
    weight_old = 1.0 / sharpness
    direction = inverse_diag * residual / midpoint
    solution = solution + direction
    residual = residual - apply_fn(direction)
    for step_id in range(steps - 1):
        weight_new = 1.0 / (2.0 * sharpness - weight_old)
        direction = weight_new * weight_old * direction + (2.0 * weight_new / halfwidth) * (inverse_diag * residual)
        solution = solution + direction
        residual = residual - apply_fn(direction)
        weight_old = weight_new
    return solution, residual


def pad_groups(array, starts):
    cont = jnp.where(starts[..., 1:] == 0, 1.0, 0.0)
    closed = jnp.zeros_like(cont[..., :1])
    lower = jnp.concatenate([closed, cont], axis=-1)[..., None, None, None]
    upper = jnp.concatenate([cont, closed], axis=-1)[..., None, None, None]
    below = jnp.concatenate([jnp.zeros_like(array[..., :1, :, :1, :]), array[..., :-1, :, -1:, :]], axis=-4) * lower
    above = jnp.concatenate([array[..., 1:, :, :1, :], jnp.zeros_like(array[..., :1, :, :1, :])], axis=-4) * upper
    joined = jnp.concatenate([below, array, above], axis=-2)
    widths = [(0, 0)] * (joined.ndim - 3) + [(1, 1), (0, 0), (1, 1)]
    return jnp.pad(joined, widths)


def same_group(starts):
    count = starts.shape[-1]
    marks = jnp.where(jnp.arange(count, dtype=jnp.int32) > 0, starts, 0).astype(jnp.int32)
    labels = jnp.cumsum(marks, axis=-1).astype(jnp.int32)
    return jnp.where(labels[..., :, None] == labels[..., None, :], 1.0, 0.0).astype(jnp.float32)


def reference(rhs_field, shear_modulus, lame_lambda, group_start):
    mu_pad = jnp.pad(shear_modulus, 1)
    lam_pad = jnp.pad(lame_lambda, 1)
    inverse_diag = 1.0 / diagonal(mu_pad, lam_pad, 1.0)

    def fine_apply(field):
        return operate(jnp.pad(field, ((0, 0), (1, 1), (1, 1), (1, 1))), mu_pad, lam_pad, 1.0)

    solution, residual = smooth(jnp.zeros_like(rhs_field), rhs_field, inverse_diag, fine_apply, SWEEPS)
    coarse_res = residual.reshape(3, NX // 2, 2, NY // 2, 2, NZ // 2, 2).sum(axis=(2, 4, 6))
    coarse_mu = shear_modulus.reshape(NX // 2, 2, NY // 2, 2, NZ // 2, 2).mean(axis=(1, 3, 5))
    coarse_lam = lame_lambda.reshape(NX // 2, 2, NY // 2, 2, NZ // 2, 2).mean(axis=(1, 3, 5))

    def to_blocks(array):
        return array.reshape(array.shape[0], N_GX, CX // 2, N_GY, CY // 2, NZ // 2).transpose(0, 1, 3, 2, 4, 5)

    res_blocks = to_blocks(coarse_res)
    coef_pad = pad_groups(to_blocks(jnp.stack([coarse_mu, coarse_lam])), group_start)
    coarse_inverse = 1.0 / diagonal(coef_pad[0], coef_pad[1], 4.0)

    def coarse_apply(field):
        return operate(pad_groups(field, group_start), coef_pad[0], coef_pad[1], 4.0)

    correction, coarse_left = smooth(jnp.zeros_like(res_blocks), res_blocks, coarse_inverse, coarse_apply, COARSE_SWEEPS)
    device_sums = res_blocks.sum(axis=(3, 4, 5))
    members = same_group(group_start)
    totals = jnp.einsum("gij,cgj->cgi", members, device_sums)
    cells_dev = (CX // 2) * (CY // 2) * (NZ // 2)
    group_cells = members.sum(axis=-1) * cells_dev
    group_shift = totals / (SHIFT_SCALE * group_cells[None])
    correction = correction + group_shift[:, :, :, None, None, None]
    correction = correction.transpose(0, 1, 3, 2, 4, 5).reshape(3, NX // 2, NY // 2, NZ // 2)
    fine_corr = jnp.broadcast_to(correction[:, :, None, :, None, :, None], (3, NX // 2, 2, NY // 2, 2, NZ // 2, 2)).reshape(3, NX, NY, NZ)
    solution = solution + fine_corr
    residual = residual - fine_apply(fine_corr)
    solution, residual = smooth(solution, residual, inverse_diag, fine_apply, SWEEPS)
    return solution, residual
```

```python
import jax
import jax.numpy as jnp
from jax import lax
from jax.sharding import PartitionSpec as P

SWEEPS = 3
COARSE_SWEEPS = 4


LOW_BOUND = 0.5
HIGH_BOUND = 6.0
SHIFT_SCALE = 48.0
UNITS = ((1, 0, 0), (0, 1, 0), (0, 0, 1))


def shifted(array, step_x, step_y, step_z):
    size_x = array.shape[-3] - 2
    size_y = array.shape[-2] - 2
    size_z = array.shape[-1] - 2
    return array[
        ...,
        1 + step_x : 1 + step_x + size_x,
        1 + step_y : 1 + step_y + size_y,
        1 + step_z : 1 + step_z + size_z,
    ]


def diagonal(mu_pad, lam_pad, scale):
    mu_centre = shifted(mu_pad, 0, 0, 0)
    lam_centre = shifted(lam_pad, 0, 0, 0)
    faces = 0.0
    for unit in UNITS:
        backward = tuple((-value for value in unit))
        faces = (
            faces
            + 0.5 * (mu_centre + shifted(mu_pad, *unit))
            + 0.5 * (mu_centre + shifted(mu_pad, *backward))
        )
    results = []
    for unit in UNITS:
        backward = tuple((-value for value in unit))
        results.append(scale * (faces + lam_centre + shifted(lam_pad, *backward)))
    return jnp.stack(results)


def operate(field_pad, mu_pad, lam_pad, scale):
    mu_centre = shifted(mu_pad, 0, 0, 0)
    lam_centre = shifted(lam_pad, 0, 0, 0)
    components = [field_pad[0], field_pad[1], field_pad[2]]
    centres = [shifted(value, 0, 0, 0) for value in components]
    laplace = [0.0, 0.0, 0.0]
    for unit in UNITS:
        backward = tuple((-value for value in unit))
        face_up = 0.5 * (mu_centre + shifted(mu_pad, *unit))
        face_down = 0.5 * (mu_centre + shifted(mu_pad, *backward))
        for comp_id in range(3):
            laplace[comp_id] = (
                laplace[comp_id]
                + face_up * (shifted(components[comp_id], *unit) - centres[comp_id])
                - face_down * (centres[comp_id] - shifted(components[comp_id], *backward))
            )

    def spread(offset):
        total = 0.0
        for comp_id in range(3):
            ahead = tuple((offset[axis_id] + UNITS[comp_id][axis_id] for axis_id in range(3)))
            total = total + (
                shifted(components[comp_id], *ahead) - shifted(components[comp_id], *offset)
            )
        return total

    stress_here = lam_centre * spread((0, 0, 0))
    results = []
    for comp_id in range(3):
        backward = tuple((-value for value in UNITS[comp_id]))
        grad_term = stress_here - shifted(lam_pad, *backward) * spread(backward)
        results.append(scale * (-laplace[comp_id] - grad_term))
    return jnp.stack(results)


def smooth(solution, residual, inverse_diag, apply_fn, steps):
    midpoint = 0.5 * (HIGH_BOUND + LOW_BOUND)
    halfwidth = 0.5 * (HIGH_BOUND - LOW_BOUND)
    sharpness = midpoint / halfwidth
    weight_old = 1.0 / sharpness
    direction = inverse_diag * residual / midpoint
    solution = solution + direction
    residual = residual - apply_fn(direction)
    for step_id in range(steps - 1):
        weight_new = 1.0 / (2.0 * sharpness - weight_old)
        direction = weight_new * weight_old * direction + 2.0 * weight_new / halfwidth * (
            inverse_diag * residual
        )
        solution = solution + direction
        residual = residual - apply_fn(direction)
        weight_old = weight_new
    return (solution, residual)


def pad_groups(array, starts):
    cont = jnp.where(starts[..., 1:] == 0, 1.0, 0.0)
    closed = jnp.zeros_like(cont[..., :1])
    lower = jnp.concatenate([closed, cont], axis=-1)[..., None, None, None]
    upper = jnp.concatenate([cont, closed], axis=-1)[..., None, None, None]
    below = (
        jnp.concatenate(
            [jnp.zeros_like(array[..., :1, :, :1, :]), array[..., :-1, :, -1:, :]], axis=-4
        )
        * lower
    )
    above = (
        jnp.concatenate(
            [array[..., 1:, :, :1, :], jnp.zeros_like(array[..., :1, :, :1, :])], axis=-4
        )
        * upper
    )
    joined = jnp.concatenate([below, array, above], axis=-2)
    widths = [(0, 0)] * (joined.ndim - 3) + [(1, 1), (0, 0), (1, 1)]
    return jnp.pad(joined, widths)


def same_group(starts):
    count = starts.shape[-1]
    marks = jnp.where(jnp.arange(count, dtype=jnp.int32) > 0, starts, 0)
    labels = jnp.cumsum(marks, axis=-1)
    return jnp.where(labels[..., :, None] == labels[..., None, :], 1.0, 0.0).astype(jnp.float32)


def crop(array, cut):
    if cut == 0:
        return array
    return array[..., cut:-cut, cut:-cut, :]


def shifted_ext(array, step_x, step_y, step_z):
    size_x = array.shape[-3] - 2
    size_y = array.shape[-2] - 2
    inner = array[..., 1 + step_x : 1 + step_x + size_x, 1 + step_y : 1 + step_y + size_y, :]
    if step_z == 0:
        return inner
    zero = jnp.zeros_like(inner[..., :1])
    if step_z > 0:
        return jnp.concatenate([inner[..., 1:], zero], axis=-1)
    return jnp.concatenate([zero, inner[..., :-1]], axis=-1)


def diagonal_ext(mu_pad, lam_pad, scale):
    mu_centre = shifted_ext(mu_pad, 0, 0, 0)
    lam_centre = shifted_ext(lam_pad, 0, 0, 0)
    faces = 0.0
    for unit in UNITS:
        backward = tuple((-value for value in unit))
        faces = (
            faces
            + 0.5 * (mu_centre + shifted_ext(mu_pad, *unit))
            + 0.5 * (mu_centre + shifted_ext(mu_pad, *backward))
        )
    results = []
    for unit in UNITS:
        backward = tuple((-value for value in unit))
        results.append(scale * (faces + lam_centre + shifted_ext(lam_pad, *backward)))
    return jnp.stack(results)


def apply_ext(field_pad, mu_pad, lam_pad, scale):
    mu_centre = shifted_ext(mu_pad, 0, 0, 0)
    lam_centre = shifted_ext(lam_pad, 0, 0, 0)
    components = [field_pad[0], field_pad[1], field_pad[2]]
    centres = [shifted_ext(value, 0, 0, 0) for value in components]
    laplace = [0.0, 0.0, 0.0]
    for unit in UNITS:
        backward = tuple((-value for value in unit))
        face_up = 0.5 * (mu_centre + shifted_ext(mu_pad, *unit))
        face_down = 0.5 * (mu_centre + shifted_ext(mu_pad, *backward))
        for comp_id in range(3):
            laplace[comp_id] = (
                laplace[comp_id]
                + face_up * (shifted_ext(components[comp_id], *unit) - centres[comp_id])
                - face_down * (centres[comp_id] - shifted_ext(components[comp_id], *backward))
            )

    def spread(offset):
        total = 0.0
        for comp_id in range(3):
            ahead = tuple((offset[axis_id] + UNITS[comp_id][axis_id] for axis_id in range(3)))
            total = total + (
                shifted_ext(components[comp_id], *ahead)
                - shifted_ext(components[comp_id], *offset)
            )
        return total

    stress_here = lam_centre * spread((0, 0, 0))
    results = []
    for comp_id in range(3):
        backward = tuple((-value for value in UNITS[comp_id]))
        grad_term = stress_here - shifted_ext(lam_pad, *backward) * spread(backward)
        results.append(scale * (-laplace[comp_id] - grad_term))
    return jnp.stack(results)


def halo_x(parts):
    count = lax.axis_size("gx")
    reach = max((d + a.shape[-3] - 1) // a.shape[-3] for a, d in parts)
    lows = [[] for _ in parts]
    highs = [[] for _ in parts]
    for dx in range(reach, 0, -1):
        send_low, send_high, keys = [], [], []
        for index, (array, d) in enumerate(parts):
            width = array.shape[-3]
            need = min(width, d - (dx - 1) * width)
            if need <= 0:
                continue
            keys.append((index, array.shape[:-3] + (need,) + array.shape[-2:]))
            send_low.append(array[..., width - need :, :, :].reshape(-1))
            send_high.append(array[..., :need, :, :].reshape(-1))
        forward = [(i, i + dx) for i in range(count - dx)]
        backward = [(i + dx, i) for i in range(count - dx)]
        got_low = lax.ppermute(jnp.concatenate(send_low), "gx", forward)
        got_high = lax.ppermute(jnp.concatenate(send_high), "gx", backward)
        offset = 0
        for index, shape in keys:
            size = 1
            for value in shape:
                size *= value
            lows[index].append(got_low[offset : offset + size].reshape(shape))
            highs[index].append(got_high[offset : offset + size].reshape(shape))
            offset += size
    out = []
    for index, (array, d) in enumerate(parts):
        out.append(jnp.concatenate(lows[index] + [array] + highs[index][::-1], axis=-3))
    return out


def halo_y(array, depth):
    count = lax.axis_size("gy")
    forward = [(i, i + 1) for i in range(count - 1)]
    backward = [(i + 1, i) for i in range(count - 1)]
    low = lax.ppermute(array[..., -depth:, :], "gy", forward)
    high = lax.ppermute(array[..., :depth, :], "gy", backward)
    return jnp.concatenate([low, array, high], axis=-2)


def inside_mask(width_x, width_y, depth):
    gx = lax.axis_index("gx")
    gy = lax.axis_index("gy")
    total_x = width_x * lax.axis_size("gx")
    total_y = width_y * lax.axis_size("gy")
    xs = gx * width_x + jnp.arange(width_x + 2 * depth) - depth
    ys = gy * width_y + jnp.arange(width_y + 2 * depth) - depth
    ok_x = (xs >= 0) & (xs < total_x)
    ok_y = (ys >= 0) & (ys < total_y)
    return (ok_x[:, None] & ok_y[None, :])[:, :, None]


def smooth_ext(solution, residual, inverse_diag, mu, lam, depth, steps):
    midpoint = 0.5 * (HIGH_BOUND + LOW_BOUND)
    halfwidth = 0.5 * (HIGH_BOUND - LOW_BOUND)
    sharpness = midpoint / halfwidth
    weight_old = 1.0 / sharpness
    level = depth
    direction = inverse_diag * residual / midpoint
    solution = solution + crop(direction, level)
    cut = depth + 1 - level
    residual = crop(residual, 1) - apply_ext(direction, crop(mu, cut), crop(lam, cut), 1.0)
    level -= 1
    for step_id in range(steps - 1):
        weight_new = 1.0 / (2.0 * sharpness - weight_old)
        direction = weight_new * weight_old * crop(direction, 1) + 2.0 * weight_new / halfwidth * (
            crop(inverse_diag, depth - level) * residual
        )
        solution = solution + crop(direction, level)
        cut = depth + 1 - level
        residual = crop(residual, 1) - apply_ext(direction, crop(mu, cut), crop(lam, cut), 1.0)
        level -= 1
        weight_old = weight_new
    return (solution, residual)


def pair_matrix(coarse_z):
    fine = jnp.arange(2 * coarse_z) // 2
    return (fine[None, :] == jnp.arange(coarse_z)[:, None]).astype(jnp.float32)


def upsample_z(array, pairs):
    return jnp.einsum("...k,kj->...j", array, pairs, precision=lax.Precision.HIGHEST)


def restrict_z(array, pairs):
    return jnp.einsum("...j,kj->...k", array, pairs, precision=lax.Precision.HIGHEST)


def shards(rhs_field, shear_modulus, lame_lambda, group_start):
    width_x = rhs_field.shape[1]
    width_y = rhs_field.shape[2]
    width_z = rhs_field.shape[3]
    depth = SWEEPS
    gy = lax.axis_index("gy")
    count_y = lax.axis_size("gy")

    stacked = jnp.concatenate([rhs_field, shear_modulus[None], lame_lambda[None]], axis=0)
    (stacked,) = halo_x([(stacked, depth + 1)])
    stacked = halo_y(stacked, depth + 1)
    mu_ext = stacked[3]
    lam_ext = stacked[4]
    rhs_ext = crop(stacked[0:3], 1)
    inside = inside_mask(width_x, width_y, depth)
    inverse_diag = jnp.where(inside[None], 1.0 / diagonal_ext(mu_ext, lam_ext, 1.0), 0.0)

    solution, residual = smooth_ext(
        jnp.zeros_like(rhs_field), rhs_ext, inverse_diag, mu_ext, lam_ext, depth, SWEEPS
    )
    coarse_x = width_x // 2
    coarse_y = width_y // 2
    coarse_z = width_z // 2
    pairs = pair_matrix(coarse_z)
    coarse_res = restrict_z(residual, pairs).reshape(3, coarse_x, 2, coarse_y, 2, coarse_z)
    coarse_res = coarse_res.sum(axis=(2, 4))
    coarse_coef = restrict_z(jnp.stack([shear_modulus, lame_lambda]), pairs)
    coarse_coef = coarse_coef.reshape(2, coarse_x, 2, coarse_y, 2, coarse_z).sum(axis=(2, 4)) / 8.0
    coarse_mu = coarse_coef[0]
    coarse_lam = coarse_coef[1]
    starts = group_start[0]
    members = same_group(starts)
    cells_dev = coarse_x * coarse_y * coarse_z

    edge_low = residual[:, :, :depth, :]
    edge_high = residual[:, :, -depth:, :]
    coarse_pack = jnp.concatenate([coarse_res, coarse_mu[None], coarse_lam[None]], axis=0)
    package = jnp.concatenate(
        [coarse_pack.reshape(-1), edge_low.reshape(-1), edge_high.reshape(-1)]
    )
    column = lax.all_gather(package, "gy", axis=0, tiled=False)
    coarse_size = coarse_pack.size
    edge_size = edge_low.size
    column_pack = column[:, :coarse_size].reshape((count_y,) + coarse_pack.shape)
    column_pack = jnp.moveaxis(column_pack, 0, 1)
    column_low = column[:, coarse_size : coarse_size + edge_size].reshape(
        (count_y,) + edge_low.shape
    )
    column_high = column[:, coarse_size + edge_size :].reshape((count_y,) + edge_high.shape)
    below = lax.dynamic_index_in_dim(column_high, jnp.maximum(gy - 1, 0), 0, keepdims=False)
    above = lax.dynamic_index_in_dim(
        column_low, jnp.minimum(gy + 1, count_y - 1), 0, keepdims=False
    )
    below = jnp.where(gy > 0, below, 0.0)
    above = jnp.where(gy < count_y - 1, above, 0.0)
    residual_y = jnp.concatenate([below, residual, above], axis=2)

    coef_pad = pad_groups(column_pack[3:5], starts)
    coarse_inverse = 1.0 / diagonal(coef_pad[0], coef_pad[1], 4.0)

    def coarse_apply(field):
        return operate(pad_groups(field, starts), coef_pad[0], coef_pad[1], 4.0)

    column_res = column_pack[0:3]
    smoothed, coarse_left = smooth(
        jnp.zeros_like(column_res), column_res, coarse_inverse, coarse_apply, COARSE_SWEEPS
    )
    device_sums = column_res.sum(axis=(2, 3, 4))
    totals = jnp.sum(device_sums[:, None, :] * members[None, :, :], axis=2)
    group_cells = jnp.sum(members, axis=1) * cells_dev
    group_shift = totals / (SHIFT_SCALE * group_cells[None, :])
    correction = smoothed + group_shift[:, :, None, None, None]
    correction = jnp.moveaxis(correction, 1, 2).reshape(3, coarse_x, count_y * coarse_y, coarse_z)
    reach_c = (depth + 2) // 2
    correction = jnp.pad(correction, ((0, 0), (0, 0), (reach_c, reach_c), (0, 0)))
    corr_y = lax.dynamic_slice_in_dim(correction, gy * coarse_y, coarse_y + 2 * reach_c, axis=2)

    residual_ext, corr_ext = halo_x([(residual_y, depth), (corr_y, reach_c)])
    corr_z = upsample_z(corr_ext, pairs)
    fine_corr = jnp.broadcast_to(
        corr_z[:, :, None, :, None, :],
        (3, corr_ext.shape[1], 2, corr_ext.shape[2], 2, width_z),
    ).reshape(3, 2 * corr_ext.shape[1], 2 * corr_ext.shape[2], width_z)
    fine_depth = 2 * reach_c
    fine_corr = crop(fine_corr, fine_depth - (depth + 1))
    solution = solution + crop(fine_corr, depth + 1)
    residual_ext = residual_ext - apply_ext(fine_corr, mu_ext, lam_ext, 1.0)
    solution, residual = smooth_ext(
        solution, residual_ext, inverse_diag, mu_ext, lam_ext, depth, SWEEPS
    )
    return (solution, residual)


def solution(mesh):
    return jax.shard_map(
        shards,
        mesh=mesh,
        in_specs=(
            P(None, "gx", "gy", None),
            P("gx", "gy", None),
            P("gx", "gy", None),
            P("gx", None),
        ),
        out_specs=(P(None, "gx", "gy", None), P(None, "gx", "gy", None)),
        check_vma=False,
    )
```

```python
import jax
import jax.numpy as jnp
from jax import lax
from jax.sharding import PartitionSpec as P

SWEEPS = 3
COARSE_SWEEPS = 4


LOW_BOUND = 0.5
HIGH_BOUND = 6.0
SHIFT_SCALE = 48.0
UNITS = ((1, 0, 0), (0, 1, 0), (0, 0, 1))


def shifted(array, step_x, step_y, step_z):
    size_x = array.shape[-3] - 2
    size_y = array.shape[-2] - 2
    size_z = array.shape[-1] - 2
    return array[
        ...,
        1 + step_x : 1 + step_x + size_x,
        1 + step_y : 1 + step_y + size_y,
        1 + step_z : 1 + step_z + size_z,
    ]


def diagonal(mu_pad, lam_pad, scale):
    mu_centre = shifted(mu_pad, 0, 0, 0)
    lam_centre = shifted(lam_pad, 0, 0, 0)
    faces = 0.0
    for unit in UNITS:
        backward = tuple((-value for value in unit))
        faces = (
            faces
            + 0.5 * (mu_centre + shifted(mu_pad, *unit))
            + 0.5 * (mu_centre + shifted(mu_pad, *backward))
        )
    results = []
    for unit in UNITS:
        backward = tuple((-value for value in unit))
        results.append(scale * (faces + lam_centre + shifted(lam_pad, *backward)))
    return jnp.stack(results)


def operate(field_pad, mu_pad, lam_pad, scale):
    mu_centre = shifted(mu_pad, 0, 0, 0)
    lam_centre = shifted(lam_pad, 0, 0, 0)
    components = [field_pad[0], field_pad[1], field_pad[2]]
    centres = [shifted(value, 0, 0, 0) for value in components]
    laplace = [0.0, 0.0, 0.0]
    for unit in UNITS:
        backward = tuple((-value for value in unit))
        face_up = 0.5 * (mu_centre + shifted(mu_pad, *unit))
        face_down = 0.5 * (mu_centre + shifted(mu_pad, *backward))
        for comp_id in range(3):
            laplace[comp_id] = (
                laplace[comp_id]
                + face_up * (shifted(components[comp_id], *unit) - centres[comp_id])
                - face_down * (centres[comp_id] - shifted(components[comp_id], *backward))
            )

    def spread(offset):
        total = 0.0
        for comp_id in range(3):
            ahead = tuple((offset[axis_id] + UNITS[comp_id][axis_id] for axis_id in range(3)))
            total = total + (
                shifted(components[comp_id], *ahead) - shifted(components[comp_id], *offset)
            )
        return total

    stress_here = lam_centre * spread((0, 0, 0))
    results = []
    for comp_id in range(3):
        backward = tuple((-value for value in UNITS[comp_id]))
        grad_term = stress_here - shifted(lam_pad, *backward) * spread(backward)
        results.append(scale * (-laplace[comp_id] - grad_term))
    return jnp.stack(results)


def smooth(solution, residual, inverse_diag, apply_fn, steps):
    midpoint = 0.5 * (HIGH_BOUND + LOW_BOUND)
    halfwidth = 0.5 * (HIGH_BOUND - LOW_BOUND)
    sharpness = midpoint / halfwidth
    weight_old = 1.0 / sharpness
    direction = inverse_diag * residual / midpoint
    solution = solution + direction
    residual = residual - apply_fn(direction)
    for step_id in range(steps - 1):
        weight_new = 1.0 / (2.0 * sharpness - weight_old)
        direction = weight_new * weight_old * direction + 2.0 * weight_new / halfwidth * (
            inverse_diag * residual
        )
        solution = solution + direction
        residual = residual - apply_fn(direction)
        weight_old = weight_new
    return (solution, residual)


def pad_groups(array, starts):
    cont = jnp.where(starts[..., 1:] == 0, 1.0, 0.0)
    closed = jnp.zeros_like(cont[..., :1])
    lower = jnp.concatenate([closed, cont], axis=-1)[..., None, None, None]
    upper = jnp.concatenate([cont, closed], axis=-1)[..., None, None, None]
    below = (
        jnp.concatenate(
            [jnp.zeros_like(array[..., :1, :, :1, :]), array[..., :-1, :, -1:, :]], axis=-4
        )
        * lower
    )
    above = (
        jnp.concatenate(
            [array[..., 1:, :, :1, :], jnp.zeros_like(array[..., :1, :, :1, :])], axis=-4
        )
        * upper
    )
    joined = jnp.concatenate([below, array, above], axis=-2)
    widths = [(0, 0)] * (joined.ndim - 3) + [(1, 1), (0, 0), (1, 1)]
    return jnp.pad(joined, widths)


def same_group(starts):
    count = starts.shape[-1]
    marks = jnp.where(jnp.arange(count, dtype=jnp.int32) > 0, starts, 0)
    labels = jnp.cumsum(marks, axis=-1)
    return jnp.where(labels[..., :, None] == labels[..., None, :], 1.0, 0.0).astype(jnp.float32)


def crop(array, cut):
    if cut == 0:
        return array
    return array[..., cut:-cut, cut:-cut, :]


def shifted_ext(array, step_x, step_y, step_z):
    size_x = array.shape[-3] - 2
    size_y = array.shape[-2] - 2
    inner = array[..., 1 + step_x : 1 + step_x + size_x, 1 + step_y : 1 + step_y + size_y, :]
    if step_z == 0:
        return inner
    zero = jnp.zeros_like(inner[..., :1])
    if step_z > 0:
        return jnp.concatenate([inner[..., 1:], zero], axis=-1)
    return jnp.concatenate([zero, inner[..., :-1]], axis=-1)


def diagonal_ext(mu_pad, lam_pad, scale):
    mu_centre = shifted_ext(mu_pad, 0, 0, 0)
    lam_centre = shifted_ext(lam_pad, 0, 0, 0)
    faces = 0.0
    for unit in UNITS:
        backward = tuple((-value for value in unit))
        faces = (
            faces
            + 0.5 * (mu_centre + shifted_ext(mu_pad, *unit))
            + 0.5 * (mu_centre + shifted_ext(mu_pad, *backward))
        )
    results = []
    for unit in UNITS:
        backward = tuple((-value for value in unit))
        results.append(scale * (faces + lam_centre + shifted_ext(lam_pad, *backward)))
    return jnp.stack(results)


def apply_ext(field_pad, mu_pad, lam_pad, scale):
    mu_centre = shifted_ext(mu_pad, 0, 0, 0)
    lam_centre = shifted_ext(lam_pad, 0, 0, 0)
    components = [field_pad[0], field_pad[1], field_pad[2]]
    centres = [shifted_ext(value, 0, 0, 0) for value in components]
    laplace = [0.0, 0.0, 0.0]
    for unit in UNITS:
        backward = tuple((-value for value in unit))
        face_up = 0.5 * (mu_centre + shifted_ext(mu_pad, *unit))
        face_down = 0.5 * (mu_centre + shifted_ext(mu_pad, *backward))
        for comp_id in range(3):
            laplace[comp_id] = (
                laplace[comp_id]
                + face_up * (shifted_ext(components[comp_id], *unit) - centres[comp_id])
                - face_down * (centres[comp_id] - shifted_ext(components[comp_id], *backward))
            )

    def spread(offset):
        total = 0.0
        for comp_id in range(3):
            ahead = tuple((offset[axis_id] + UNITS[comp_id][axis_id] for axis_id in range(3)))
            total = total + (
                shifted_ext(components[comp_id], *ahead)
                - shifted_ext(components[comp_id], *offset)
            )
        return total

    stress_here = lam_centre * spread((0, 0, 0))
    results = []
    for comp_id in range(3):
        backward = tuple((-value for value in UNITS[comp_id]))
        grad_term = stress_here - shifted_ext(lam_pad, *backward) * spread(backward)
        results.append(scale * (-laplace[comp_id] - grad_term))
    return jnp.stack(results)


def halo_x(array, depth):
    count = lax.axis_size("gx")
    width = array.shape[-3]
    reach = (depth + width - 1) // width
    lows, highs = [], []
    for dx in range(reach, 0, -1):
        need = min(width, depth - (dx - 1) * width)
        forward = [(i, i + dx) for i in range(count - dx)]
        backward = [(i + dx, i) for i in range(count - dx)]
        lows.append(lax.ppermute(array[..., width - need :, :, :], "gx", forward))
        highs.append(lax.ppermute(array[..., :need, :, :], "gx", backward))
    return jnp.concatenate(lows + [array] + highs[::-1], axis=-3)


def halo_y(array, depth):
    count = lax.axis_size("gy")
    forward = [(i, i + 1) for i in range(count - 1)]
    backward = [(i + 1, i) for i in range(count - 1)]
    low = lax.ppermute(array[..., -depth:, :], "gy", forward)
    high = lax.ppermute(array[..., :depth, :], "gy", backward)
    return jnp.concatenate([low, array, high], axis=-2)


def inside_mask(width_x, width_y, depth):
    gx = lax.axis_index("gx")
    gy = lax.axis_index("gy")
    total_x = width_x * lax.axis_size("gx")
    total_y = width_y * lax.axis_size("gy")
    xs = gx * width_x + jnp.arange(width_x + 2 * depth) - depth
    ys = gy * width_y + jnp.arange(width_y + 2 * depth) - depth
    ok_x = (xs >= 0) & (xs < total_x)
    ok_y = (ys >= 0) & (ys < total_y)
    return (ok_x[:, None] & ok_y[None, :])[:, :, None]


def smooth_ext(solution, residual, inverse_diag, mu, lam, depth, steps):
    midpoint = 0.5 * (HIGH_BOUND + LOW_BOUND)
    halfwidth = 0.5 * (HIGH_BOUND - LOW_BOUND)
    sharpness = midpoint / halfwidth
    weight_old = 1.0 / sharpness
    level = depth
    direction = inverse_diag * residual / midpoint
    solution = solution + crop(direction, level)
    cut = depth + 1 - level
    residual = crop(residual, 1) - apply_ext(direction, crop(mu, cut), crop(lam, cut), 1.0)
    level -= 1
    for step_id in range(steps - 1):
        weight_new = 1.0 / (2.0 * sharpness - weight_old)
        direction = weight_new * weight_old * crop(direction, 1) + 2.0 * weight_new / halfwidth * (
            crop(inverse_diag, depth - level) * residual
        )
        solution = solution + crop(direction, level)
        cut = depth + 1 - level
        residual = crop(residual, 1) - apply_ext(direction, crop(mu, cut), crop(lam, cut), 1.0)
        level -= 1
        weight_old = weight_new
    return (solution, residual)


def pair_matrix(coarse_z):
    fine = jnp.arange(2 * coarse_z) // 2
    return (fine[None, :] == jnp.arange(coarse_z)[:, None]).astype(jnp.float32)


def upsample_z(array, pairs):
    return jnp.einsum("...k,kj->...j", array, pairs, precision=lax.Precision.HIGHEST)


def restrict_z(array, pairs):
    return jnp.einsum("...j,kj->...k", array, pairs, precision=lax.Precision.HIGHEST)


def shards(rhs_field, shear_modulus, lame_lambda, group_start):
    width_x = rhs_field.shape[1]
    width_y = rhs_field.shape[2]
    width_z = rhs_field.shape[3]
    depth = SWEEPS
    gy = lax.axis_index("gy")
    count_y = lax.axis_size("gy")

    stacked = jnp.concatenate([rhs_field, shear_modulus[None], lame_lambda[None]], axis=0)
    stacked = halo_x(stacked, depth + 1)
    stacked = halo_y(stacked, depth + 1)
    mu_ext = stacked[3]
    lam_ext = stacked[4]
    rhs_ext = crop(stacked[0:3], 1)
    inside = inside_mask(width_x, width_y, depth)
    inverse_diag = jnp.where(inside[None], 1.0 / diagonal_ext(mu_ext, lam_ext, 1.0), 0.0)

    solution, residual = smooth_ext(
        jnp.zeros_like(rhs_field), rhs_ext, inverse_diag, mu_ext, lam_ext, depth, SWEEPS
    )
    coarse_x = width_x // 2
    coarse_y = width_y // 2
    coarse_z = width_z // 2
    pairs = pair_matrix(coarse_z)
    coarse_res = restrict_z(residual, pairs).reshape(3, coarse_x, 2, coarse_y, 2, coarse_z)
    coarse_res = coarse_res.sum(axis=(2, 4))
    coarse_coef = restrict_z(jnp.stack([shear_modulus, lame_lambda]), pairs)
    coarse_coef = coarse_coef.reshape(2, coarse_x, 2, coarse_y, 2, coarse_z).sum(axis=(2, 4)) / 8.0
    coarse_mu = coarse_coef[0]
    coarse_lam = coarse_coef[1]
    starts = group_start[0]
    members = same_group(starts)
    cells_dev = coarse_x * coarse_y * coarse_z

    sums = coarse_res.sum(axis=(1, 2, 3))
    slots = jnp.where(jnp.arange(count_y)[:, None] == gy, sums[None, :], 0.0)
    all_sums = lax.psum(slots, "gy")

    forward = [(i, i + 1) for i in range(count_y - 1)]
    backward = [(i + 1, i) for i in range(count_y - 1)]
    fine_reach = depth + 1
    below = lax.ppermute(residual[:, :, -fine_reach:, :], "gy", forward)
    above = lax.ppermute(residual[:, :, :fine_reach, :], "gy", backward)
    coarse_pack = jnp.concatenate([coarse_res, coarse_mu[None], coarse_lam[None]], axis=0)
    pack_below = lax.ppermute(coarse_pack, "gy", forward)
    pack_above = lax.ppermute(coarse_pack, "gy", backward)
    residual_y = jnp.concatenate([below, residual, above], axis=2)

    window = jnp.stack([pack_below, coarse_pack, pack_above], axis=1)
    next_start = lax.dynamic_index_in_dim(starts, jnp.minimum(gy + 1, count_y - 1), 0, keepdims=False)
    own_start = lax.dynamic_index_in_dim(starts, gy, 0, keepdims=False)
    window_starts = jnp.stack([jnp.zeros_like(own_start), own_start, next_start])
    coef_pad = pad_groups(window[3:5], window_starts)
    coarse_diag = diagonal(coef_pad[0], coef_pad[1], 4.0)
    owners = gy - 1 + jnp.arange(3)
    valid = (owners >= 0) & (owners < count_y)
    usable = valid[None, :, None, None, None] & (coarse_diag > 0.0)
    coarse_inverse = jnp.where(usable, 1.0 / coarse_diag, 0.0)

    def coarse_apply(field):
        return operate(pad_groups(field, window_starts), coef_pad[0], coef_pad[1], 4.0)

    window_res = window[0:3]
    smoothed, coarse_left = smooth(
        jnp.zeros_like(window_res), window_res, coarse_inverse, coarse_apply, COARSE_SWEEPS
    )
    totals = jnp.sum(members[:, :, None] * all_sums[None, :, :], axis=1)
    group_cells = jnp.sum(members, axis=1) * cells_dev
    group_shift = totals / (SHIFT_SCALE * group_cells[:, None])
    window_shift = jnp.take(group_shift, jnp.clip(owners, 0, count_y - 1), axis=0)
    window_shift = jnp.where(valid[:, None], window_shift, 0.0)
    correction = smoothed + window_shift.T[:, :, None, None, None]
    correction = jnp.moveaxis(correction, 1, 2).reshape(3, coarse_x, 3 * coarse_y, coarse_z)
    reach_c = (depth + 2) // 2
    corr_y = correction[:, :, coarse_y - reach_c : 2 * coarse_y + reach_c, :]
    corr_z = upsample_z(corr_y, pairs)
    fine_corr = jnp.broadcast_to(
        corr_z[:, :, None, :, None, :],
        (3, coarse_x, 2, corr_y.shape[2], 2, width_z),
    ).reshape(3, width_x, 2 * corr_y.shape[2], width_z)
    fine_depth = 2 * reach_c
    fine_corr = fine_corr[:, :, fine_depth - fine_reach : fine_corr.shape[2] - (fine_depth - fine_reach), :]

    joined = halo_x(jnp.concatenate([residual_y, fine_corr], axis=0), fine_reach)
    residual_ext = crop(joined[0:3], 1)
    fine_corr = joined[3:6]
    solution = solution + crop(fine_corr, fine_reach)
    residual_ext = residual_ext - apply_ext(fine_corr, mu_ext, lam_ext, 1.0)
    solution, residual = smooth_ext(
        solution, residual_ext, inverse_diag, mu_ext, lam_ext, depth, SWEEPS
    )
    return (solution, residual)


def solution(mesh):
    return jax.shard_map(
        shards,
        mesh=mesh,
        in_specs=(
            P(None, "gx", "gy", None),
            P("gx", "gy", None),
            P("gx", "gy", None),
            P("gx", None),
        ),
        out_specs=(P(None, "gx", "gy", None), P(None, "gx", "gy", None)),
        check_vma=False,
    )
```

```python
import jax
import jax.numpy as jnp
from jax import lax
from jax.sharding import PartitionSpec as P

SWEEPS = 3
COARSE_SWEEPS = 4


LOW_BOUND = 0.5
HIGH_BOUND = 6.0
SHIFT_SCALE = 48.0
UNITS = ((1, 0, 0), (0, 1, 0), (0, 0, 1))


def shifted(array, step_x, step_y, step_z):
    size_x = array.shape[-3] - 2
    size_y = array.shape[-2] - 2
    size_z = array.shape[-1] - 2
    return array[
        ...,
        1 + step_x : 1 + step_x + size_x,
        1 + step_y : 1 + step_y + size_y,
        1 + step_z : 1 + step_z + size_z,
    ]


def diagonal(mu_pad, lam_pad, scale):
    mu_centre = shifted(mu_pad, 0, 0, 0)
    lam_centre = shifted(lam_pad, 0, 0, 0)
    faces = 0.0
    for unit in UNITS:
        backward = tuple((-value for value in unit))
        faces = (
            faces
            + 0.5 * (mu_centre + shifted(mu_pad, *unit))
            + 0.5 * (mu_centre + shifted(mu_pad, *backward))
        )
    results = []
    for unit in UNITS:
        backward = tuple((-value for value in unit))
        results.append(scale * (faces + lam_centre + shifted(lam_pad, *backward)))
    return jnp.stack(results)


def operate(field_pad, mu_pad, lam_pad, scale):
    mu_centre = shifted(mu_pad, 0, 0, 0)
    lam_centre = shifted(lam_pad, 0, 0, 0)
    components = [field_pad[0], field_pad[1], field_pad[2]]
    centres = [shifted(value, 0, 0, 0) for value in components]
    laplace = [0.0, 0.0, 0.0]
    for unit in UNITS:
        backward = tuple((-value for value in unit))
        face_up = 0.5 * (mu_centre + shifted(mu_pad, *unit))
        face_down = 0.5 * (mu_centre + shifted(mu_pad, *backward))
        for comp_id in range(3):
            laplace[comp_id] = (
                laplace[comp_id]
                + face_up * (shifted(components[comp_id], *unit) - centres[comp_id])
                - face_down * (centres[comp_id] - shifted(components[comp_id], *backward))
            )

    def spread(offset):
        total = 0.0
        for comp_id in range(3):
            ahead = tuple((offset[axis_id] + UNITS[comp_id][axis_id] for axis_id in range(3)))
            total = total + (
                shifted(components[comp_id], *ahead) - shifted(components[comp_id], *offset)
            )
        return total

    stress_here = lam_centre * spread((0, 0, 0))
    results = []
    for comp_id in range(3):
        backward = tuple((-value for value in UNITS[comp_id]))
        grad_term = stress_here - shifted(lam_pad, *backward) * spread(backward)
        results.append(scale * (-laplace[comp_id] - grad_term))
    return jnp.stack(results)


def smooth(solution, residual, inverse_diag, apply_fn, steps):
    midpoint = 0.5 * (HIGH_BOUND + LOW_BOUND)
    halfwidth = 0.5 * (HIGH_BOUND - LOW_BOUND)
    sharpness = midpoint / halfwidth
    weight_old = 1.0 / sharpness
    direction = inverse_diag * residual / midpoint
    solution = solution + direction
    residual = residual - apply_fn(direction)
    for step_id in range(steps - 1):
        weight_new = 1.0 / (2.0 * sharpness - weight_old)
        direction = weight_new * weight_old * direction + 2.0 * weight_new / halfwidth * (
            inverse_diag * residual
        )
        solution = solution + direction
        residual = residual - apply_fn(direction)
        weight_old = weight_new
    return (solution, residual)


def pad_groups(array, starts):
    cont = jnp.where(starts[..., 1:] == 0, 1.0, 0.0)
    closed = jnp.zeros_like(cont[..., :1])
    lower = jnp.concatenate([closed, cont], axis=-1)[..., None, None, None]
    upper = jnp.concatenate([cont, closed], axis=-1)[..., None, None, None]
    below = (
        jnp.concatenate(
            [jnp.zeros_like(array[..., :1, :, :1, :]), array[..., :-1, :, -1:, :]], axis=-4
        )
        * lower
    )
    above = (
        jnp.concatenate(
            [array[..., 1:, :, :1, :], jnp.zeros_like(array[..., :1, :, :1, :])], axis=-4
        )
        * upper
    )
    joined = jnp.concatenate([below, array, above], axis=-2)
    widths = [(0, 0)] * (joined.ndim - 3) + [(1, 1), (0, 0), (1, 1)]
    return jnp.pad(joined, widths)


def same_group(starts):
    count = starts.shape[-1]
    marks = jnp.where(jnp.arange(count, dtype=jnp.int32) > 0, starts, 0)
    labels = jnp.cumsum(marks, axis=-1)
    return jnp.where(labels[..., :, None] == labels[..., None, :], 1.0, 0.0).astype(jnp.float32)


def crop(array, cut):
    if cut == 0:
        return array
    return array[..., cut:-cut, cut:-cut, :]


def shifted_ext(array, step_x, step_y, step_z):
    size_x = array.shape[-3] - 2
    size_y = array.shape[-2] - 2
    inner = array[..., 1 + step_x : 1 + step_x + size_x, 1 + step_y : 1 + step_y + size_y, :]
    if step_z == 0:
        return inner
    zero = jnp.zeros_like(inner[..., :1])
    if step_z > 0:
        return jnp.concatenate([inner[..., 1:], zero], axis=-1)
    return jnp.concatenate([zero, inner[..., :-1]], axis=-1)


def diagonal_ext(mu_pad, lam_pad, scale):
    mu_centre = shifted_ext(mu_pad, 0, 0, 0)
    lam_centre = shifted_ext(lam_pad, 0, 0, 0)
    faces = 0.0
    for unit in UNITS:
        backward = tuple((-value for value in unit))
        faces = (
            faces
            + 0.5 * (mu_centre + shifted_ext(mu_pad, *unit))
            + 0.5 * (mu_centre + shifted_ext(mu_pad, *backward))
        )
    results = []
    for unit in UNITS:
        backward = tuple((-value for value in unit))
        results.append(scale * (faces + lam_centre + shifted_ext(lam_pad, *backward)))
    return jnp.stack(results)


def apply_ext(field_pad, mu_pad, lam_pad, scale):
    mu_centre = shifted_ext(mu_pad, 0, 0, 0)
    lam_centre = shifted_ext(lam_pad, 0, 0, 0)
    components = [field_pad[0], field_pad[1], field_pad[2]]
    centres = [shifted_ext(value, 0, 0, 0) for value in components]
    laplace = [0.0, 0.0, 0.0]
    for unit in UNITS:
        backward = tuple((-value for value in unit))
        face_up = 0.5 * (mu_centre + shifted_ext(mu_pad, *unit))
        face_down = 0.5 * (mu_centre + shifted_ext(mu_pad, *backward))
        for comp_id in range(3):
            laplace[comp_id] = (
                laplace[comp_id]
                + face_up * (shifted_ext(components[comp_id], *unit) - centres[comp_id])
                - face_down * (centres[comp_id] - shifted_ext(components[comp_id], *backward))
            )

    def spread(offset):
        total = 0.0
        for comp_id in range(3):
            ahead = tuple((offset[axis_id] + UNITS[comp_id][axis_id] for axis_id in range(3)))
            total = total + (
                shifted_ext(components[comp_id], *ahead)
                - shifted_ext(components[comp_id], *offset)
            )
        return total

    stress_here = lam_centre * spread((0, 0, 0))
    results = []
    for comp_id in range(3):
        backward = tuple((-value for value in UNITS[comp_id]))
        grad_term = stress_here - shifted_ext(lam_pad, *backward) * spread(backward)
        results.append(scale * (-laplace[comp_id] - grad_term))
    return jnp.stack(results)


def halo_x(array, depth):
    count = lax.axis_size("gx")
    width = array.shape[-3]
    reach = (depth + width - 1) // width
    lows, highs = [], []
    for dx in range(reach, 0, -1):
        need = min(width, depth - (dx - 1) * width)
        forward = [(i, i + dx) for i in range(count - dx)]
        backward = [(i + dx, i) for i in range(count - dx)]
        lows.append(lax.ppermute(array[..., width - need :, :, :], "gx", forward))
        highs.append(lax.ppermute(array[..., :need, :, :], "gx", backward))
    return jnp.concatenate(lows + [array] + highs[::-1], axis=-3)


def halo_y(array, depth):
    count = lax.axis_size("gy")
    forward = [(i, i + 1) for i in range(count - 1)]
    backward = [(i + 1, i) for i in range(count - 1)]
    low = lax.ppermute(array[..., -depth:, :], "gy", forward)
    high = lax.ppermute(array[..., :depth, :], "gy", backward)
    return jnp.concatenate([low, array, high], axis=-2)


def inside_mask(width_x, width_y, depth):
    gx = lax.axis_index("gx")
    gy = lax.axis_index("gy")
    total_x = width_x * lax.axis_size("gx")
    total_y = width_y * lax.axis_size("gy")
    xs = gx * width_x + jnp.arange(width_x + 2 * depth) - depth
    ys = gy * width_y + jnp.arange(width_y + 2 * depth) - depth
    ok_x = (xs >= 0) & (xs < total_x)
    ok_y = (ys >= 0) & (ys < total_y)
    return (ok_x[:, None] & ok_y[None, :])[:, :, None]


def smooth_ext(solution, residual, inverse_diag, mu, lam, depth, steps):
    midpoint = 0.5 * (HIGH_BOUND + LOW_BOUND)
    halfwidth = 0.5 * (HIGH_BOUND - LOW_BOUND)
    sharpness = midpoint / halfwidth
    weight_old = 1.0 / sharpness
    level = depth
    direction = inverse_diag * residual / midpoint
    solution = solution + crop(direction, level)
    cut = depth + 1 - level
    residual = crop(residual, 1) - apply_ext(direction, crop(mu, cut), crop(lam, cut), 1.0)
    level -= 1
    for step_id in range(steps - 1):
        weight_new = 1.0 / (2.0 * sharpness - weight_old)
        direction = weight_new * weight_old * crop(direction, 1) + 2.0 * weight_new / halfwidth * (
            crop(inverse_diag, depth - level) * residual
        )
        solution = solution + crop(direction, level)
        cut = depth + 1 - level
        residual = crop(residual, 1) - apply_ext(direction, crop(mu, cut), crop(lam, cut), 1.0)
        level -= 1
        weight_old = weight_new
    return (solution, residual)


def pair_matrix(coarse_z):
    fine = jnp.arange(2 * coarse_z) // 2
    return (fine[None, :] == jnp.arange(coarse_z)[:, None]).astype(jnp.float32)


def upsample_z(array, pairs):
    return jnp.einsum("...k,kj->...j", array, pairs, precision=lax.Precision.HIGHEST)


def restrict_z(array, pairs):
    return jnp.einsum("...j,kj->...k", array, pairs, precision=lax.Precision.HIGHEST)


def shards(rhs_field, shear_modulus, lame_lambda, group_start):
    width_x = rhs_field.shape[1]
    width_y = rhs_field.shape[2]
    width_z = rhs_field.shape[3]
    depth = SWEEPS
    gy = lax.axis_index("gy")
    count_y = lax.axis_size("gy")

    stacked = jnp.concatenate([rhs_field, shear_modulus[None], lame_lambda[None]], axis=0)
    stacked = halo_x(stacked, depth + 1)
    stacked = halo_y(stacked, depth + 1)
    mu_ext = stacked[3]
    lam_ext = stacked[4]
    rhs_ext = crop(stacked[0:3], 1)
    inside = inside_mask(width_x, width_y, depth)
    inverse_diag = jnp.where(inside[None], 1.0 / diagonal_ext(mu_ext, lam_ext, 1.0), 0.0)

    solution, residual = smooth_ext(
        jnp.zeros_like(rhs_field), rhs_ext, inverse_diag, mu_ext, lam_ext, depth, SWEEPS
    )
    coarse_x = width_x // 2
    coarse_y = width_y // 2
    coarse_z = width_z // 2
    pairs = pair_matrix(coarse_z)
    coarse_res = restrict_z(residual, pairs).reshape(3, coarse_x, 2, coarse_y, 2, coarse_z)
    coarse_res = coarse_res.sum(axis=(2, 4))
    coarse_coef = restrict_z(jnp.stack([shear_modulus, lame_lambda]), pairs)
    coarse_coef = coarse_coef.reshape(2, coarse_x, 2, coarse_y, 2, coarse_z).sum(axis=(2, 4)) / 8.0
    coarse_mu = coarse_coef[0]
    coarse_lam = coarse_coef[1]
    starts = group_start[0]
    members = same_group(starts)
    cells_dev = coarse_x * coarse_y * coarse_z

    sums = coarse_res.sum(axis=(1, 2, 3))
    gathered = sums[None, :]
    while gathered.shape[0] < count_y:
        have = gathered.shape[0]
        take = min(have, count_y - have)
        ring = [(i, (i + have) % count_y) for i in range(count_y)]
        gathered = jnp.concatenate([gathered, lax.ppermute(gathered[:take], "gy", ring)], axis=0)
    all_sums = jnp.take(gathered, (gy - jnp.arange(count_y)) % count_y, axis=0)

    forward = [(i, i + 1) for i in range(count_y - 1)]
    backward = [(i + 1, i) for i in range(count_y - 1)]
    fine_reach = depth + 1
    below = lax.ppermute(residual[:, :, -fine_reach:, :], "gy", forward)
    above = lax.ppermute(residual[:, :, :fine_reach, :], "gy", backward)
    coarse_pack = jnp.concatenate([coarse_res, coarse_mu[None], coarse_lam[None]], axis=0)
    pack_below = lax.ppermute(coarse_pack, "gy", forward)
    pack_above = lax.ppermute(coarse_pack, "gy", backward)
    residual_y = jnp.concatenate([below, residual, above], axis=2)

    window = jnp.stack([pack_below, coarse_pack, pack_above], axis=1)
    next_start = lax.dynamic_index_in_dim(starts, jnp.minimum(gy + 1, count_y - 1), 0, keepdims=False)
    own_start = lax.dynamic_index_in_dim(starts, gy, 0, keepdims=False)
    window_starts = jnp.stack([jnp.zeros_like(own_start), own_start, next_start])
    coef_pad = pad_groups(window[3:5], window_starts)
    coarse_diag = diagonal(coef_pad[0], coef_pad[1], 4.0)
    owners = gy - 1 + jnp.arange(3)
    valid = (owners >= 0) & (owners < count_y)
    usable = valid[None, :, None, None, None] & (coarse_diag > 0.0)
    coarse_inverse = jnp.where(usable, 1.0 / coarse_diag, 0.0)

    def coarse_apply(field):
        return operate(pad_groups(field, window_starts), coef_pad[0], coef_pad[1], 4.0)

    window_res = window[0:3]
    smoothed, coarse_left = smooth(
        jnp.zeros_like(window_res), window_res, coarse_inverse, coarse_apply, COARSE_SWEEPS
    )
    totals = jnp.sum(members[:, :, None] * all_sums[None, :, :], axis=1)
    group_cells = jnp.sum(members, axis=1) * cells_dev
    group_shift = totals / (SHIFT_SCALE * group_cells[:, None])
    window_shift = jnp.take(group_shift, jnp.clip(owners, 0, count_y - 1), axis=0)
    window_shift = jnp.where(valid[:, None], window_shift, 0.0)
    correction = smoothed + window_shift.T[:, :, None, None, None]
    correction = jnp.moveaxis(correction, 1, 2).reshape(3, coarse_x, 3 * coarse_y, coarse_z)
    reach_c = (depth + 2) // 2
    corr_y = correction[:, :, coarse_y - reach_c : 2 * coarse_y + reach_c, :]
    corr_z = upsample_z(corr_y, pairs)
    fine_corr = jnp.broadcast_to(
        corr_z[:, :, None, :, None, :],
        (3, coarse_x, 2, corr_y.shape[2], 2, width_z),
    ).reshape(3, width_x, 2 * corr_y.shape[2], width_z)
    fine_depth = 2 * reach_c
    fine_corr = fine_corr[:, :, fine_depth - fine_reach : fine_corr.shape[2] - (fine_depth - fine_reach), :]

    joined = halo_x(jnp.concatenate([residual_y, fine_corr], axis=0), fine_reach)
    residual_ext = crop(joined[0:3], 1)
    fine_corr = joined[3:6]
    solution = solution + crop(fine_corr, fine_reach)
    residual_ext = residual_ext - apply_ext(fine_corr, mu_ext, lam_ext, 1.0)
    solution, residual = smooth_ext(
        solution, residual_ext, inverse_diag, mu_ext, lam_ext, depth, SWEEPS
    )
    return (solution, residual)


def solution(mesh):
    return jax.shard_map(
        shards,
        mesh=mesh,
        in_specs=(
            P(None, "gx", "gy", None),
            P("gx", "gy", None),
            P("gx", "gy", None),
            P("gx", None),
        ),
        out_specs=(P(None, "gx", "gy", None), P(None, "gx", "gy", None)),
        check_vma=False,
    )
```

```python
import jax
import jax.numpy as jnp
from jax import lax
from jax.sharding import PartitionSpec as P

SWEEPS = 3
COARSE_SWEEPS = 4


LOW_BOUND = 0.5
HIGH_BOUND = 6.0
SHIFT_SCALE = 48.0
UNITS = ((1, 0, 0), (0, 1, 0), (0, 0, 1))


def shifted(array, step_x, step_y, step_z):
    size_x = array.shape[-3] - 2
    size_y = array.shape[-2] - 2
    size_z = array.shape[-1] - 2
    return array[
        ...,
        1 + step_x : 1 + step_x + size_x,
        1 + step_y : 1 + step_y + size_y,
        1 + step_z : 1 + step_z + size_z,
    ]


def diagonal(mu_pad, lam_pad, scale):
    mu_centre = shifted(mu_pad, 0, 0, 0)
    lam_centre = shifted(lam_pad, 0, 0, 0)
    faces = 0.0
    for unit in UNITS:
        backward = tuple((-value for value in unit))
        faces = (
            faces
            + 0.5 * (mu_centre + shifted(mu_pad, *unit))
            + 0.5 * (mu_centre + shifted(mu_pad, *backward))
        )
    results = []
    for unit in UNITS:
        backward = tuple((-value for value in unit))
        results.append(scale * (faces + lam_centre + shifted(lam_pad, *backward)))
    return jnp.stack(results)


def operate(field_pad, mu_pad, lam_pad, scale):
    mu_centre = shifted(mu_pad, 0, 0, 0)
    lam_centre = shifted(lam_pad, 0, 0, 0)
    components = [field_pad[0], field_pad[1], field_pad[2]]
    centres = [shifted(value, 0, 0, 0) for value in components]
    laplace = [0.0, 0.0, 0.0]
    for unit in UNITS:
        backward = tuple((-value for value in unit))
        face_up = 0.5 * (mu_centre + shifted(mu_pad, *unit))
        face_down = 0.5 * (mu_centre + shifted(mu_pad, *backward))
        for comp_id in range(3):
            laplace[comp_id] = (
                laplace[comp_id]
                + face_up * (shifted(components[comp_id], *unit) - centres[comp_id])
                - face_down * (centres[comp_id] - shifted(components[comp_id], *backward))
            )

    def spread(offset):
        total = 0.0
        for comp_id in range(3):
            ahead = tuple((offset[axis_id] + UNITS[comp_id][axis_id] for axis_id in range(3)))
            total = total + (
                shifted(components[comp_id], *ahead) - shifted(components[comp_id], *offset)
            )
        return total

    stress_here = lam_centre * spread((0, 0, 0))
    results = []
    for comp_id in range(3):
        backward = tuple((-value for value in UNITS[comp_id]))
        grad_term = stress_here - shifted(lam_pad, *backward) * spread(backward)
        results.append(scale * (-laplace[comp_id] - grad_term))
    return jnp.stack(results)


def smooth(solution, residual, inverse_diag, apply_fn, steps):
    midpoint = 0.5 * (HIGH_BOUND + LOW_BOUND)
    halfwidth = 0.5 * (HIGH_BOUND - LOW_BOUND)
    sharpness = midpoint / halfwidth
    weight_old = 1.0 / sharpness
    direction = inverse_diag * residual / midpoint
    solution = solution + direction
    residual = residual - apply_fn(direction)
    for step_id in range(steps - 1):
        weight_new = 1.0 / (2.0 * sharpness - weight_old)
        direction = weight_new * weight_old * direction + 2.0 * weight_new / halfwidth * (
            inverse_diag * residual
        )
        solution = solution + direction
        residual = residual - apply_fn(direction)
        weight_old = weight_new
    return (solution, residual)


def pad_groups(array, starts):
    cont = jnp.where(starts[..., 1:] == 0, 1.0, 0.0)
    closed = jnp.zeros_like(cont[..., :1])
    lower = jnp.concatenate([closed, cont], axis=-1)[..., None, None, None]
    upper = jnp.concatenate([cont, closed], axis=-1)[..., None, None, None]
    below = (
        jnp.concatenate(
            [jnp.zeros_like(array[..., :1, :, :1, :]), array[..., :-1, :, -1:, :]], axis=-4
        )
        * lower
    )
    above = (
        jnp.concatenate(
            [array[..., 1:, :, :1, :], jnp.zeros_like(array[..., :1, :, :1, :])], axis=-4
        )
        * upper
    )
    joined = jnp.concatenate([below, array, above], axis=-2)
    widths = [(0, 0)] * (joined.ndim - 3) + [(1, 1), (0, 0), (1, 1)]
    return jnp.pad(joined, widths)


def same_group(starts):
    count = starts.shape[-1]
    marks = jnp.where(jnp.arange(count, dtype=jnp.int32) > 0, starts, 0)
    labels = jnp.cumsum(marks, axis=-1)
    return jnp.where(labels[..., :, None] == labels[..., None, :], 1.0, 0.0).astype(jnp.float32)


def crop(array, cut):
    if cut == 0:
        return array
    return array[..., cut:-cut, cut:-cut, :]


def shifted_ext(array, step_x, step_y, step_z):
    size_x = array.shape[-3] - 2
    size_y = array.shape[-2] - 2
    inner = array[..., 1 + step_x : 1 + step_x + size_x, 1 + step_y : 1 + step_y + size_y, :]
    if step_z == 0:
        return inner
    zero = jnp.zeros_like(inner[..., :1])
    if step_z > 0:
        return jnp.concatenate([inner[..., 1:], zero], axis=-1)
    return jnp.concatenate([zero, inner[..., :-1]], axis=-1)


def diagonal_ext(mu_pad, lam_pad, scale):
    mu_centre = shifted_ext(mu_pad, 0, 0, 0)
    lam_centre = shifted_ext(lam_pad, 0, 0, 0)
    faces = 0.0
    for unit in UNITS:
        backward = tuple((-value for value in unit))
        faces = (
            faces
            + 0.5 * (mu_centre + shifted_ext(mu_pad, *unit))
            + 0.5 * (mu_centre + shifted_ext(mu_pad, *backward))
        )
    results = []
    for unit in UNITS:
        backward = tuple((-value for value in unit))
        results.append(scale * (faces + lam_centre + shifted_ext(lam_pad, *backward)))
    return jnp.stack(results)


def apply_ext(field_pad, mu_pad, lam_pad, scale):
    mu_centre = shifted_ext(mu_pad, 0, 0, 0)
    lam_centre = shifted_ext(lam_pad, 0, 0, 0)
    components = [field_pad[0], field_pad[1], field_pad[2]]
    centres = [shifted_ext(value, 0, 0, 0) for value in components]
    laplace = [0.0, 0.0, 0.0]
    for unit in UNITS:
        backward = tuple((-value for value in unit))
        face_up = 0.5 * (mu_centre + shifted_ext(mu_pad, *unit))
        face_down = 0.5 * (mu_centre + shifted_ext(mu_pad, *backward))
        for comp_id in range(3):
            laplace[comp_id] = (
                laplace[comp_id]
                + face_up * (shifted_ext(components[comp_id], *unit) - centres[comp_id])
                - face_down * (centres[comp_id] - shifted_ext(components[comp_id], *backward))
            )

    def spread(offset):
        total = 0.0
        for comp_id in range(3):
            ahead = tuple((offset[axis_id] + UNITS[comp_id][axis_id] for axis_id in range(3)))
            total = total + (
                shifted_ext(components[comp_id], *ahead)
                - shifted_ext(components[comp_id], *offset)
            )
        return total

    stress_here = lam_centre * spread((0, 0, 0))
    results = []
    for comp_id in range(3):
        backward = tuple((-value for value in UNITS[comp_id]))
        grad_term = stress_here - shifted_ext(lam_pad, *backward) * spread(backward)
        results.append(scale * (-laplace[comp_id] - grad_term))
    return jnp.stack(results)


def halo_x(array, depth):
    count = lax.axis_size("gx")
    width = array.shape[-3]
    reach = (depth + width - 1) // width
    lows, highs = [], []
    for dx in range(reach, 0, -1):
        need = min(width, depth - (dx - 1) * width)
        forward = [(i, i + dx) for i in range(count - dx)]
        backward = [(i + dx, i) for i in range(count - dx)]
        lows.append(lax.ppermute(array[..., width - need :, :, :], "gx", forward))
        highs.append(lax.ppermute(array[..., :need, :, :], "gx", backward))
    return jnp.concatenate(lows + [array] + highs[::-1], axis=-3)


def halo_y(array, depth):
    count = lax.axis_size("gy")
    forward = [(i, i + 1) for i in range(count - 1)]
    backward = [(i + 1, i) for i in range(count - 1)]
    low = lax.ppermute(array[..., -depth:, :], "gy", forward)
    high = lax.ppermute(array[..., :depth, :], "gy", backward)
    return jnp.concatenate([low, array, high], axis=-2)


def inside_mask(width_x, width_y, depth):
    gx = lax.axis_index("gx")
    gy = lax.axis_index("gy")
    total_x = width_x * lax.axis_size("gx")
    total_y = width_y * lax.axis_size("gy")
    xs = gx * width_x + jnp.arange(width_x + 2 * depth) - depth
    ys = gy * width_y + jnp.arange(width_y + 2 * depth) - depth
    ok_x = (xs >= 0) & (xs < total_x)
    ok_y = (ys >= 0) & (ys < total_y)
    return (ok_x[:, None] & ok_y[None, :])[:, :, None]


def smooth_ext(solution, residual, inverse_diag, mu, lam, depth, steps):
    midpoint = 0.5 * (HIGH_BOUND + LOW_BOUND)
    halfwidth = 0.5 * (HIGH_BOUND - LOW_BOUND)
    sharpness = midpoint / halfwidth
    weight_old = 1.0 / sharpness
    level = depth
    direction = inverse_diag * residual / midpoint
    solution = solution + crop(direction, level)
    cut = depth + 1 - level
    residual = crop(residual, 1) - apply_ext(direction, crop(mu, cut), crop(lam, cut), 1.0)
    level -= 1
    for step_id in range(steps - 1):
        weight_new = 1.0 / (2.0 * sharpness - weight_old)
        direction = weight_new * weight_old * crop(direction, 1) + 2.0 * weight_new / halfwidth * (
            crop(inverse_diag, depth - level) * residual
        )
        solution = solution + crop(direction, level)
        cut = depth + 1 - level
        residual = crop(residual, 1) - apply_ext(direction, crop(mu, cut), crop(lam, cut), 1.0)
        level -= 1
        weight_old = weight_new
    return (solution, residual)


def pair_matrix(coarse_z):
    fine = jnp.arange(2 * coarse_z) // 2
    return (fine[None, :] == jnp.arange(coarse_z)[:, None]).astype(jnp.float32)


def upsample_z(array, pairs):
    return jnp.einsum("...k,kj->...j", array, pairs, precision=lax.Precision.HIGHEST)


def restrict_z(array, pairs):
    return jnp.einsum("...j,kj->...k", array, pairs, precision=lax.Precision.HIGHEST)


def shards(rhs_field, shear_modulus, lame_lambda, group_start):
    width_x = rhs_field.shape[1]
    width_y = rhs_field.shape[2]
    width_z = rhs_field.shape[3]
    depth = SWEEPS
    gy = lax.axis_index("gy")
    count_y = lax.axis_size("gy")

    stacked = jnp.concatenate([rhs_field, shear_modulus[None], lame_lambda[None]], axis=0)
    stacked = halo_x(stacked, depth + 1)
    stacked = halo_y(stacked, depth + 1)
    mu_ext = stacked[3]
    lam_ext = stacked[4]
    rhs_ext = crop(stacked[0:3], 1)
    inside = inside_mask(width_x, width_y, depth)
    inverse_diag = jnp.where(inside[None], 1.0 / diagonal_ext(mu_ext, lam_ext, 1.0), 0.0)

    solution, residual = smooth_ext(
        jnp.zeros_like(rhs_field), rhs_ext, inverse_diag, mu_ext, lam_ext, depth, SWEEPS
    )
    coarse_x = width_x // 2
    coarse_y = width_y // 2
    coarse_z = width_z // 2
    pairs = pair_matrix(coarse_z)
    coarse_res = restrict_z(residual, pairs).reshape(3, coarse_x, 2, coarse_y, 2, coarse_z)
    coarse_res = coarse_res.sum(axis=(2, 4))
    coarse_coef = restrict_z(jnp.stack([shear_modulus, lame_lambda]), pairs)
    coarse_coef = coarse_coef.reshape(2, coarse_x, 2, coarse_y, 2, coarse_z).sum(axis=(2, 4)) / 8.0
    coarse_mu = coarse_coef[0]
    coarse_lam = coarse_coef[1]
    starts = group_start[0]
    members = same_group(starts)
    cells_dev = coarse_x * coarse_y * coarse_z

    count_x = lax.axis_size("gx")
    sums = coarse_res.sum(axis=(1, 2, 3))
    own_info = jnp.concatenate([sums, starts.astype(jnp.float32)])
    side = (depth + 2) // 2
    lows, highs = [], []
    for dx in range(side, 0, -1):
        lows.append(lax.ppermute(own_info, "gx", [(i, i + dx) for i in range(count_x - dx)]))
        highs.append(lax.ppermute(own_info, "gx", [(i + dx, i) for i in range(count_x - dx)]))
    column_info = jnp.stack(lows + [own_info] + highs[::-1])
    slots = jnp.where(
        jnp.arange(count_y)[None, :, None] == gy, column_info[:, None, :3], 0.0
    )
    all_sums = lax.psum(slots, "gy")
    column_starts = jnp.round(column_info[:, 3:]).astype(jnp.int32)

    forward = [(i, i + 1) for i in range(count_y - 1)]
    backward = [(i + 1, i) for i in range(count_y - 1)]
    fine_reach = depth + 1
    below = lax.ppermute(residual[:, :, -fine_reach:, :], "gy", forward)
    above = lax.ppermute(residual[:, :, :fine_reach, :], "gy", backward)
    coarse_pack = jnp.concatenate([coarse_res, coarse_mu[None], coarse_lam[None]], axis=0)
    pack_below = lax.ppermute(coarse_pack, "gy", forward)
    pack_above = lax.ppermute(coarse_pack, "gy", backward)
    residual_y = jnp.concatenate([below, residual, above], axis=2)

    window = jnp.stack([pack_below, coarse_pack, pack_above], axis=1)
    next_start = lax.dynamic_index_in_dim(starts, jnp.minimum(gy + 1, count_y - 1), 0, keepdims=False)
    own_start = lax.dynamic_index_in_dim(starts, gy, 0, keepdims=False)
    window_starts = jnp.stack([jnp.zeros_like(own_start), own_start, next_start])
    coef_pad = pad_groups(window[3:5], window_starts)
    coarse_diag = diagonal(coef_pad[0], coef_pad[1], 4.0)
    owners = gy - 1 + jnp.arange(3)
    valid = (owners >= 0) & (owners < count_y)
    usable = valid[None, :, None, None, None] & (coarse_diag > 0.0)
    coarse_inverse = jnp.where(usable, 1.0 / coarse_diag, 0.0)

    def coarse_apply(field):
        return operate(pad_groups(field, window_starts), coef_pad[0], coef_pad[1], 4.0)

    window_res = window[0:3]
    smoothed, coarse_left = smooth(
        jnp.zeros_like(window_res), window_res, coarse_inverse, coarse_apply, COARSE_SWEEPS
    )
    correction = smoothed
    correction = jnp.moveaxis(correction, 1, 2).reshape(3, coarse_x, 3 * coarse_y, coarse_z)
    reach_c = (depth + 2) // 2
    corr_y = correction[:, :, coarse_y - reach_c : 2 * coarse_y + reach_c, :]
    corr_z = upsample_z(corr_y, pairs)
    fine_corr = jnp.broadcast_to(
        corr_z[:, :, None, :, None, :],
        (3, coarse_x, 2, corr_y.shape[2], 2, width_z),
    ).reshape(3, width_x, 2 * corr_y.shape[2], width_z)
    fine_depth = 2 * reach_c
    fine_corr = fine_corr[:, :, fine_depth - fine_reach : fine_corr.shape[2] - (fine_depth - fine_reach), :]

    joined = halo_x(jnp.concatenate([residual_y, fine_corr], axis=0), fine_reach)
    residual_ext = crop(joined[0:3], 1)
    fine_corr = joined[3:6]

    column_members = same_group(column_starts)
    totals = jnp.sum(column_members[:, :, :, None] * all_sums[:, None, :, :], axis=2)
    group_cells = jnp.sum(column_members, axis=2) * cells_dev
    group_shift = totals / (SHIFT_SCALE * group_cells[:, :, None])
    columns = lax.axis_index("gx") + jnp.arange(-side, side + 1)
    column_ok = (columns >= 0) & (columns < count_x)
    owners = gy - 1 + jnp.arange(3)
    owner_ok = (owners >= 0) & (owners < count_y)
    block_shift = jnp.take(group_shift, jnp.clip(owners, 0, count_y - 1), axis=1)
    block_shift = jnp.where(column_ok[:, None, None] & owner_ok[None, :, None], block_shift, 0.0)
    block_shift = jnp.repeat(jnp.moveaxis(block_shift, 2, 0), 2, axis=1)
    block_shift = block_shift[:, 2 * side - fine_reach : block_shift.shape[1] - (2 * side - fine_reach)]
    rows = jnp.array([fine_reach, width_y, fine_reach])
    block_shift = jnp.repeat(block_shift, rows, axis=2, total_repeat_length=width_y + 2 * fine_reach)
    fine_corr = fine_corr + block_shift[:, :, :, None]
    solution = solution + crop(fine_corr, fine_reach)
    residual_ext = residual_ext - apply_ext(fine_corr, mu_ext, lam_ext, 1.0)
    solution, residual = smooth_ext(
        solution, residual_ext, inverse_diag, mu_ext, lam_ext, depth, SWEEPS
    )
    return (solution, residual)


def solution(mesh):
    return jax.shard_map(
        shards,
        mesh=mesh,
        in_specs=(
            P(None, "gx", "gy", None),
            P("gx", "gy", None),
            P("gx", "gy", None),
            P("gx", None),
        ),
        out_specs=(P(None, "gx", "gy", None), P(None, "gx", "gy", None)),
        check_vma=False,
    )
```

```python
import jax
import jax.numpy as jnp
from jax import lax
from jax.sharding import PartitionSpec as P

SWEEPS = 3
COARSE_SWEEPS = 4


LOW_BOUND = 0.5
HIGH_BOUND = 6.0
SHIFT_SCALE = 48.0
UNITS = ((1, 0, 0), (0, 1, 0), (0, 0, 1))


def shifted(array, step_x, step_y, step_z):
    size_x = array.shape[-3] - 2
    size_y = array.shape[-2] - 2
    size_z = array.shape[-1] - 2
    return array[
        ...,
        1 + step_x : 1 + step_x + size_x,
        1 + step_y : 1 + step_y + size_y,
        1 + step_z : 1 + step_z + size_z,
    ]


def diagonal(mu_pad, lam_pad, scale):
    mu_centre = shifted(mu_pad, 0, 0, 0)
    lam_centre = shifted(lam_pad, 0, 0, 0)
    faces = 0.0
    for unit in UNITS:
        backward = tuple((-value for value in unit))
        faces = (
            faces
            + 0.5 * (mu_centre + shifted(mu_pad, *unit))
            + 0.5 * (mu_centre + shifted(mu_pad, *backward))
        )
    results = []
    for unit in UNITS:
        backward = tuple((-value for value in unit))
        results.append(scale * (faces + lam_centre + shifted(lam_pad, *backward)))
    return jnp.stack(results)


def operate(field_pad, mu_pad, lam_pad, scale):
    mu_centre = shifted(mu_pad, 0, 0, 0)
    lam_centre = shifted(lam_pad, 0, 0, 0)
    components = [field_pad[0], field_pad[1], field_pad[2]]
    centres = [shifted(value, 0, 0, 0) for value in components]
    laplace = [0.0, 0.0, 0.0]
    for unit in UNITS:
        backward = tuple((-value for value in unit))
        face_up = 0.5 * (mu_centre + shifted(mu_pad, *unit))
        face_down = 0.5 * (mu_centre + shifted(mu_pad, *backward))
        for comp_id in range(3):
            laplace[comp_id] = (
                laplace[comp_id]
                + face_up * (shifted(components[comp_id], *unit) - centres[comp_id])
                - face_down * (centres[comp_id] - shifted(components[comp_id], *backward))
            )

    def spread(offset):
        total = 0.0
        for comp_id in range(3):
            ahead = tuple((offset[axis_id] + UNITS[comp_id][axis_id] for axis_id in range(3)))
            total = total + (
                shifted(components[comp_id], *ahead) - shifted(components[comp_id], *offset)
            )
        return total

    stress_here = lam_centre * spread((0, 0, 0))
    results = []
    for comp_id in range(3):
        backward = tuple((-value for value in UNITS[comp_id]))
        grad_term = stress_here - shifted(lam_pad, *backward) * spread(backward)
        results.append(scale * (-laplace[comp_id] - grad_term))
    return jnp.stack(results)


def smooth(solution, residual, inverse_diag, apply_fn, steps):
    midpoint = 0.5 * (HIGH_BOUND + LOW_BOUND)
    halfwidth = 0.5 * (HIGH_BOUND - LOW_BOUND)
    sharpness = midpoint / halfwidth
    weight_old = 1.0 / sharpness
    direction = inverse_diag * residual / midpoint
    solution = solution + direction
    residual = residual - apply_fn(direction)
    for step_id in range(steps - 1):
        weight_new = 1.0 / (2.0 * sharpness - weight_old)
        direction = weight_new * weight_old * direction + 2.0 * weight_new / halfwidth * (
            inverse_diag * residual
        )
        solution = solution + direction
        residual = residual - apply_fn(direction)
        weight_old = weight_new
    return (solution, residual)


def pad_groups(array, starts):
    cont = jnp.where(starts[..., 1:] == 0, 1.0, 0.0)
    closed = jnp.zeros_like(cont[..., :1])
    lower = jnp.concatenate([closed, cont], axis=-1)[..., None, None, None]
    upper = jnp.concatenate([cont, closed], axis=-1)[..., None, None, None]
    below = (
        jnp.concatenate(
            [jnp.zeros_like(array[..., :1, :, :1, :]), array[..., :-1, :, -1:, :]], axis=-4
        )
        * lower
    )
    above = (
        jnp.concatenate(
            [array[..., 1:, :, :1, :], jnp.zeros_like(array[..., :1, :, :1, :])], axis=-4
        )
        * upper
    )
    joined = jnp.concatenate([below, array, above], axis=-2)
    widths = [(0, 0)] * (joined.ndim - 3) + [(1, 1), (0, 0), (1, 1)]
    return jnp.pad(joined, widths)


def same_group(starts):
    count = starts.shape[-1]
    marks = jnp.where(jnp.arange(count, dtype=jnp.int32) > 0, starts, 0)
    labels = jnp.cumsum(marks, axis=-1)
    return jnp.where(labels[..., :, None] == labels[..., None, :], 1.0, 0.0).astype(jnp.float32)


def crop_xy(array, cut_x, cut_y):
    size_x = array.shape[-3]
    size_y = array.shape[-2]
    return array[..., cut_x : size_x - cut_x, cut_y : size_y - cut_y, :]


def crop(array, cut):
    if cut == 0:
        return array
    return array[..., cut:-cut, cut:-cut, :]


def shifted_ext(array, step_x, step_y, step_z):
    size_x = array.shape[-3] - 2
    size_y = array.shape[-2] - 2
    inner = array[..., 1 + step_x : 1 + step_x + size_x, 1 + step_y : 1 + step_y + size_y, :]
    if step_z == 0:
        return inner
    zero = jnp.zeros_like(inner[..., :1])
    if step_z > 0:
        return jnp.concatenate([inner[..., 1:], zero], axis=-1)
    return jnp.concatenate([zero, inner[..., :-1]], axis=-1)


def diagonal_ext(mu_pad, lam_pad, scale):
    mu_centre = shifted_ext(mu_pad, 0, 0, 0)
    lam_centre = shifted_ext(lam_pad, 0, 0, 0)
    faces = 0.0
    for unit in UNITS:
        backward = tuple((-value for value in unit))
        faces = (
            faces
            + 0.5 * (mu_centre + shifted_ext(mu_pad, *unit))
            + 0.5 * (mu_centre + shifted_ext(mu_pad, *backward))
        )
    results = []
    for unit in UNITS:
        backward = tuple((-value for value in unit))
        results.append(scale * (faces + lam_centre + shifted_ext(lam_pad, *backward)))
    return jnp.stack(results)


def apply_ext(field_pad, mu_pad, lam_pad, scale):
    mu_centre = shifted_ext(mu_pad, 0, 0, 0)
    lam_centre = shifted_ext(lam_pad, 0, 0, 0)
    components = [field_pad[0], field_pad[1], field_pad[2]]
    centres = [shifted_ext(value, 0, 0, 0) for value in components]
    laplace = [0.0, 0.0, 0.0]
    for unit in UNITS:
        backward = tuple((-value for value in unit))
        face_up = 0.5 * (mu_centre + shifted_ext(mu_pad, *unit))
        face_down = 0.5 * (mu_centre + shifted_ext(mu_pad, *backward))
        for comp_id in range(3):
            laplace[comp_id] = (
                laplace[comp_id]
                + face_up * (shifted_ext(components[comp_id], *unit) - centres[comp_id])
                - face_down * (centres[comp_id] - shifted_ext(components[comp_id], *backward))
            )

    def spread(offset):
        total = 0.0
        for comp_id in range(3):
            ahead = tuple((offset[axis_id] + UNITS[comp_id][axis_id] for axis_id in range(3)))
            total = total + (
                shifted_ext(components[comp_id], *ahead)
                - shifted_ext(components[comp_id], *offset)
            )
        return total

    stress_here = lam_centre * spread((0, 0, 0))
    results = []
    for comp_id in range(3):
        backward = tuple((-value for value in UNITS[comp_id]))
        grad_term = stress_here - shifted_ext(lam_pad, *backward) * spread(backward)
        results.append(scale * (-laplace[comp_id] - grad_term))
    return jnp.stack(results)


def halo_x(array, depth):
    count = lax.axis_size("gx")
    width = array.shape[-3]
    reach = (depth + width - 1) // width
    lows, highs = [], []
    for dx in range(reach, 0, -1):
        need = min(width, depth - (dx - 1) * width)
        forward = [(i, i + dx) for i in range(count - dx)]
        backward = [(i + dx, i) for i in range(count - dx)]
        lows.append(lax.ppermute(array[..., width - need :, :, :], "gx", forward))
        highs.append(lax.ppermute(array[..., :need, :, :], "gx", backward))
    return jnp.concatenate(lows + [array] + highs[::-1], axis=-3)


def halo_y(array, depth):
    count = lax.axis_size("gy")
    forward = [(i, i + 1) for i in range(count - 1)]
    backward = [(i + 1, i) for i in range(count - 1)]
    low = lax.ppermute(array[..., -depth:, :], "gy", forward)
    high = lax.ppermute(array[..., :depth, :], "gy", backward)
    return jnp.concatenate([low, array, high], axis=-2)


def inside_mask(width_x, width_y, depth_x, depth_y):
    gx = lax.axis_index("gx")
    gy = lax.axis_index("gy")
    total_x = width_x * lax.axis_size("gx")
    total_y = width_y * lax.axis_size("gy")
    xs = gx * width_x + jnp.arange(width_x + 2 * depth_x) - depth_x
    ys = gy * width_y + jnp.arange(width_y + 2 * depth_y) - depth_y
    ok_x = (xs >= 0) & (xs < total_x)
    ok_y = (ys >= 0) & (ys < total_y)
    return (ok_x[:, None] & ok_y[None, :])[:, :, None]


def smooth_ext(solution, residual, inverse_diag, mu, lam, steps):
    midpoint = 0.5 * (HIGH_BOUND + LOW_BOUND)
    halfwidth = 0.5 * (HIGH_BOUND - LOW_BOUND)
    sharpness = midpoint / halfwidth
    weight_old = 1.0 / sharpness

    def extent(array):
        return (
            (array.shape[-3] - solution.shape[-3]) // 2,
            (array.shape[-2] - solution.shape[-2]) // 2,
        )

    def fit(array, like):
        ax, ay = extent(array)
        bx, by = extent(like)
        return crop_xy(array, ax - bx, ay - by)

    direction = fit(inverse_diag, residual) * residual / midpoint
    solution = solution + fit(direction, solution)
    coef_like = jnp.zeros(residual.shape[-3:], residual.dtype)
    residual = crop(residual, 1) - apply_ext(direction, fit(mu, coef_like), fit(lam, coef_like), 1.0)
    for step_id in range(steps - 1):
        weight_new = 1.0 / (2.0 * sharpness - weight_old)
        direction = weight_new * weight_old * crop(direction, 1) + 2.0 * weight_new / halfwidth * (
            fit(inverse_diag, residual) * residual
        )
        solution = solution + fit(direction, solution)
        coef_like = jnp.zeros(residual.shape[-3:], residual.dtype)
        residual = crop(residual, 1) - apply_ext(
            direction, fit(mu, coef_like), fit(lam, coef_like), 1.0
        )
        weight_old = weight_new
    return (solution, residual)


def pair_matrix(coarse_z):
    fine = jnp.arange(2 * coarse_z) // 2
    return (fine[None, :] == jnp.arange(coarse_z)[:, None]).astype(jnp.float32)


def upsample_z(array, pairs):
    return jnp.einsum("...k,kj->...j", array, pairs, precision=lax.Precision.HIGHEST)


def restrict_z(array, pairs):
    return jnp.einsum("...j,kj->...k", array, pairs, precision=lax.Precision.HIGHEST)


def shards(rhs_field, shear_modulus, lame_lambda, group_start):
    width_x = rhs_field.shape[1]
    width_y = rhs_field.shape[2]
    width_z = rhs_field.shape[3]
    depth = SWEEPS
    gy = lax.axis_index("gy")
    count_y = lax.axis_size("gy")

    coarse_x = width_x // 2
    coarse_y = width_y // 2
    coarse_z = width_z // 2
    fine_reach = depth + 1
    res_rows = COARSE_SWEEPS + (depth + 2) // 2
    coef_rows = res_rows + 2
    deep_y = 2 * coef_rows

    stacked = jnp.concatenate([rhs_field, shear_modulus[None], lame_lambda[None]], axis=0)
    stacked = halo_x(stacked, depth + 1)
    stacked = halo_y(stacked, deep_y)
    mu_ext = stacked[3]
    lam_ext = stacked[4]
    rhs_ext = crop(stacked[0:3], 1)
    inside = inside_mask(width_x, width_y, depth, deep_y - 1)
    inverse_diag = jnp.where(inside[None], 1.0 / diagonal_ext(mu_ext, lam_ext, 1.0), 0.0)

    solution, residual_deep = smooth_ext(
        jnp.zeros_like(rhs_field), rhs_ext, inverse_diag, mu_ext, lam_ext, SWEEPS
    )
    deep_r = (residual_deep.shape[2] - width_y) // 2
    residual_y = crop_xy(residual_deep, 0, deep_r - fine_reach)
    pairs = pair_matrix(coarse_z)
    res_win = restrict_z(crop_xy(residual_deep, 0, deep_r - 2 * res_rows), pairs)
    res_win = res_win.reshape(3, coarse_x, 2, coarse_y + 2 * res_rows, 2, coarse_z).sum(axis=(2, 4))
    fine_coef = crop_xy(jnp.stack([mu_ext, lam_ext]), depth + 1, deep_y - 2 * coef_rows)
    coef_win = restrict_z(fine_coef, pairs)
    coef_win = coef_win.reshape(2, coarse_x, 2, coarse_y + 2 * coef_rows, 2, coarse_z)
    coef_win = coef_win.sum(axis=(2, 4)) / 8.0
    coarse_res = res_win[:, :, res_rows : res_rows + coarse_y]
    starts = group_start[0]
    members = same_group(starts)
    cells_dev = coarse_x * coarse_y * coarse_z

    sums = coarse_res.sum(axis=(1, 2, 3))
    slots = jnp.where(jnp.arange(count_y)[:, None] == gy, sums[None, :], 0.0)
    all_sums = lax.psum(slots, "gy")

    def blocks(array, rows):
        gap = jnp.zeros(array.shape[:2] + (coarse_y - rows,) + array.shape[3:], array.dtype)
        low = jnp.concatenate([gap, array[:, :, :rows]], axis=2)
        own = array[:, :, rows : rows + coarse_y]
        high = jnp.concatenate([array[:, :, rows + coarse_y :], gap], axis=2)
        return jnp.stack([low, own, high], axis=1)

    window = jnp.concatenate([blocks(res_win, res_rows), blocks(coef_win, coef_rows)], axis=0)
    next_start = lax.dynamic_index_in_dim(starts, jnp.minimum(gy + 1, count_y - 1), 0, keepdims=False)
    own_start = lax.dynamic_index_in_dim(starts, gy, 0, keepdims=False)
    window_starts = jnp.stack([jnp.zeros_like(own_start), own_start, next_start])
    coef_pad = pad_groups(window[3:5], window_starts)
    coarse_diag = diagonal(coef_pad[0], coef_pad[1], 4.0)
    owners = gy - 1 + jnp.arange(3)
    valid = (owners >= 0) & (owners < count_y)
    usable = valid[None, :, None, None, None] & (coarse_diag > 0.0)
    coarse_inverse = jnp.where(usable, 1.0 / coarse_diag, 0.0)

    def coarse_apply(field):
        return operate(pad_groups(field, window_starts), coef_pad[0], coef_pad[1], 4.0)

    window_res = window[0:3]
    smoothed, coarse_left = smooth(
        jnp.zeros_like(window_res), window_res, coarse_inverse, coarse_apply, COARSE_SWEEPS
    )
    totals = jnp.sum(members[:, :, None] * all_sums[None, :, :], axis=1)
    group_cells = jnp.sum(members, axis=1) * cells_dev
    group_shift = totals / (SHIFT_SCALE * group_cells[:, None])
    window_shift = jnp.take(group_shift, jnp.clip(owners, 0, count_y - 1), axis=0)
    window_shift = jnp.where(valid[:, None], window_shift, 0.0)
    correction = smoothed + window_shift.T[:, :, None, None, None]
    correction = jnp.moveaxis(correction, 1, 2).reshape(3, coarse_x, 3 * coarse_y, coarse_z)
    reach_c = (depth + 2) // 2
    corr_y = correction[:, :, coarse_y - reach_c : 2 * coarse_y + reach_c, :]
    corr_z = upsample_z(corr_y, pairs)
    fine_corr = jnp.broadcast_to(
        corr_z[:, :, None, :, None, :],
        (3, coarse_x, 2, corr_y.shape[2], 2, width_z),
    ).reshape(3, width_x, 2 * corr_y.shape[2], width_z)
    fine_depth = 2 * reach_c
    fine_corr = fine_corr[:, :, fine_depth - fine_reach : fine_corr.shape[2] - (fine_depth - fine_reach), :]

    joined = halo_x(jnp.concatenate([residual_y, fine_corr], axis=0), fine_reach)
    residual_ext = crop(joined[0:3], 1)
    fine_corr = joined[3:6]
    solution = solution + crop(fine_corr, fine_reach)
    coef_cut = (mu_ext.shape[-2] - fine_corr.shape[-2]) // 2
    residual_ext = residual_ext - apply_ext(
        fine_corr, crop_xy(mu_ext, 0, coef_cut), crop_xy(lam_ext, 0, coef_cut), 1.0
    )
    solution, residual = smooth_ext(
        solution, residual_ext, inverse_diag, mu_ext, lam_ext, SWEEPS
    )
    return (solution, residual)


def solution(mesh):
    return jax.shard_map(
        shards,
        mesh=mesh,
        in_specs=(
            P(None, "gx", "gy", None),
            P("gx", "gy", None),
            P("gx", "gy", None),
            P("gx", None),
        ),
        out_specs=(P(None, "gx", "gy", None), P(None, "gx", "gy", None)),
        check_vma=False,
    )
```

```python
import jax
import jax.numpy as jnp
from jax import lax
from jax.sharding import PartitionSpec as P

SWEEPS = 3
COARSE_SWEEPS = 4


LOW_BOUND = 0.5
HIGH_BOUND = 6.0
SHIFT_SCALE = 48.0
UNITS = ((1, 0, 0), (0, 1, 0), (0, 0, 1))


def shifted(array, step_x, step_y, step_z):
    size_x = array.shape[-3] - 2
    size_y = array.shape[-2] - 2
    size_z = array.shape[-1] - 2
    return array[
        ...,
        1 + step_x : 1 + step_x + size_x,
        1 + step_y : 1 + step_y + size_y,
        1 + step_z : 1 + step_z + size_z,
    ]


def diagonal(mu_pad, lam_pad, scale):
    mu_centre = shifted(mu_pad, 0, 0, 0)
    lam_centre = shifted(lam_pad, 0, 0, 0)
    faces = 0.0
    for unit in UNITS:
        backward = tuple((-value for value in unit))
        faces = (
            faces
            + 0.5 * (mu_centre + shifted(mu_pad, *unit))
            + 0.5 * (mu_centre + shifted(mu_pad, *backward))
        )
    results = []
    for unit in UNITS:
        backward = tuple((-value for value in unit))
        results.append(scale * (faces + lam_centre + shifted(lam_pad, *backward)))
    return jnp.stack(results)


def operate(field_pad, mu_pad, lam_pad, scale):
    mu_centre = shifted(mu_pad, 0, 0, 0)
    lam_centre = shifted(lam_pad, 0, 0, 0)
    components = [field_pad[0], field_pad[1], field_pad[2]]
    centres = [shifted(value, 0, 0, 0) for value in components]
    laplace = [0.0, 0.0, 0.0]
    for unit in UNITS:
        backward = tuple((-value for value in unit))
        face_up = 0.5 * (mu_centre + shifted(mu_pad, *unit))
        face_down = 0.5 * (mu_centre + shifted(mu_pad, *backward))
        for comp_id in range(3):
            laplace[comp_id] = (
                laplace[comp_id]
                + face_up * (shifted(components[comp_id], *unit) - centres[comp_id])
                - face_down * (centres[comp_id] - shifted(components[comp_id], *backward))
            )

    def spread(offset):
        total = 0.0
        for comp_id in range(3):
            ahead = tuple((offset[axis_id] + UNITS[comp_id][axis_id] for axis_id in range(3)))
            total = total + (
                shifted(components[comp_id], *ahead) - shifted(components[comp_id], *offset)
            )
        return total

    stress_here = lam_centre * spread((0, 0, 0))
    results = []
    for comp_id in range(3):
        backward = tuple((-value for value in UNITS[comp_id]))
        grad_term = stress_here - shifted(lam_pad, *backward) * spread(backward)
        results.append(scale * (-laplace[comp_id] - grad_term))
    return jnp.stack(results)


def smooth(solution, residual, inverse_diag, apply_fn, steps):
    midpoint = 0.5 * (HIGH_BOUND + LOW_BOUND)
    halfwidth = 0.5 * (HIGH_BOUND - LOW_BOUND)
    sharpness = midpoint / halfwidth
    weight_old = 1.0 / sharpness
    direction = inverse_diag * residual / midpoint
    solution = solution + direction
    residual = residual - apply_fn(direction)
    for _ in range(steps - 1):
        weight_new = 1.0 / (2.0 * sharpness - weight_old)
        direction = weight_new * weight_old * direction + 2.0 * weight_new / halfwidth * (
            inverse_diag * residual
        )
        solution = solution + direction
        residual = residual - apply_fn(direction)
        weight_old = weight_new
    return (solution, residual)


def pad_groups(array, starts):
    cont = jnp.where(starts[..., 1:] == 0, 1.0, 0.0)
    closed = jnp.zeros_like(cont[..., :1])
    lower = jnp.concatenate([closed, cont], axis=-1)[..., None, None, None]
    upper = jnp.concatenate([cont, closed], axis=-1)[..., None, None, None]
    below = (
        jnp.concatenate(
            [jnp.zeros_like(array[..., :1, :, :1, :]), array[..., :-1, :, -1:, :]], axis=-4
        )
        * lower
    )
    above = (
        jnp.concatenate(
            [array[..., 1:, :, :1, :], jnp.zeros_like(array[..., :1, :, :1, :])], axis=-4
        )
        * upper
    )
    joined = jnp.concatenate([below, array, above], axis=-2)
    widths = [(0, 0)] * (joined.ndim - 3) + [(1, 1), (0, 0), (1, 1)]
    return jnp.pad(joined, widths)


def same_group(starts):
    count = starts.shape[-1]
    marks = jnp.where(jnp.arange(count, dtype=jnp.int32) > 0, starts, 0)
    labels = jnp.cumsum(marks, axis=-1)
    return jnp.where(labels[..., :, None] == labels[..., None, :], 1.0, 0.0).astype(jnp.float32)


def crop_xy(array, cut_x, cut_y):
    size_x = array.shape[-3]
    size_y = array.shape[-2]
    return array[..., cut_x : size_x - cut_x, cut_y : size_y - cut_y, :]


def crop(array, cut):
    if cut == 0:
        return array
    return array[..., cut:-cut, cut:-cut, :]


def shifted_ext(array, step_x, step_y, step_z):
    size_x = array.shape[-3] - 2
    size_y = array.shape[-2] - 2
    inner = array[..., 1 + step_x : 1 + step_x + size_x, 1 + step_y : 1 + step_y + size_y, :]
    if step_z == 0:
        return inner
    zero = jnp.zeros_like(inner[..., :1])
    if step_z > 0:
        return jnp.concatenate([inner[..., 1:], zero], axis=-1)
    return jnp.concatenate([zero, inner[..., :-1]], axis=-1)


def diagonal_ext(mu_pad, lam_pad, scale):
    mu_centre = shifted_ext(mu_pad, 0, 0, 0)
    lam_centre = shifted_ext(lam_pad, 0, 0, 0)
    faces = 0.0
    for unit in UNITS:
        backward = tuple((-value for value in unit))
        faces = (
            faces
            + 0.5 * (mu_centre + shifted_ext(mu_pad, *unit))
            + 0.5 * (mu_centre + shifted_ext(mu_pad, *backward))
        )
    results = []
    for unit in UNITS:
        backward = tuple((-value for value in unit))
        results.append(scale * (faces + lam_centre + shifted_ext(lam_pad, *backward)))
    return jnp.stack(results)


def apply_ext(field_pad, mu_pad, lam_pad, scale):
    mu_centre = shifted_ext(mu_pad, 0, 0, 0)
    lam_centre = shifted_ext(lam_pad, 0, 0, 0)
    components = [field_pad[0], field_pad[1], field_pad[2]]
    centres = [shifted_ext(value, 0, 0, 0) for value in components]
    laplace = [0.0, 0.0, 0.0]
    for unit in UNITS:
        backward = tuple((-value for value in unit))
        face_up = 0.5 * (mu_centre + shifted_ext(mu_pad, *unit))
        face_down = 0.5 * (mu_centre + shifted_ext(mu_pad, *backward))
        for comp_id in range(3):
            laplace[comp_id] = (
                laplace[comp_id]
                + face_up * (shifted_ext(components[comp_id], *unit) - centres[comp_id])
                - face_down * (centres[comp_id] - shifted_ext(components[comp_id], *backward))
            )

    def spread(offset):
        total = 0.0
        for comp_id in range(3):
            ahead = tuple((offset[axis_id] + UNITS[comp_id][axis_id] for axis_id in range(3)))
            total = total + (
                shifted_ext(components[comp_id], *ahead)
                - shifted_ext(components[comp_id], *offset)
            )
        return total

    stress_here = lam_centre * spread((0, 0, 0))
    results = []
    for comp_id in range(3):
        backward = tuple((-value for value in UNITS[comp_id]))
        grad_term = stress_here - shifted_ext(lam_pad, *backward) * spread(backward)
        results.append(scale * (-laplace[comp_id] - grad_term))
    return jnp.stack(results)


def halo_x(array, depth):
    count = lax.axis_size("gx")
    width = array.shape[-3]
    reach = (depth + width - 1) // width
    lows, highs = [], []
    for dx in range(reach, 0, -1):
        need = min(width, depth - (dx - 1) * width)
        forward = [(i, i + dx) for i in range(count - dx)]
        backward = [(i + dx, i) for i in range(count - dx)]
        lows.append(lax.ppermute(array[..., width - need :, :, :], "gx", forward))
        highs.append(lax.ppermute(array[..., :need, :, :], "gx", backward))
    return jnp.concatenate(lows + [array] + highs[::-1], axis=-3)


def halo_y(array, depth):
    count = lax.axis_size("gy")
    forward = [(i, i + 1) for i in range(count - 1)]
    backward = [(i + 1, i) for i in range(count - 1)]
    low = lax.ppermute(array[..., -depth:, :], "gy", forward)
    high = lax.ppermute(array[..., :depth, :], "gy", backward)
    return jnp.concatenate([low, array, high], axis=-2)


def inside_mask(width_x, width_y, depth_x, depth_y):
    gx = lax.axis_index("gx")
    gy = lax.axis_index("gy")
    total_x = width_x * lax.axis_size("gx")
    total_y = width_y * lax.axis_size("gy")
    xs = gx * width_x + jnp.arange(width_x + 2 * depth_x) - depth_x
    ys = gy * width_y + jnp.arange(width_y + 2 * depth_y) - depth_y
    ok_x = (xs >= 0) & (xs < total_x)
    ok_y = (ys >= 0) & (ys < total_y)
    return (ok_x[:, None] & ok_y[None, :])[:, :, None]


def smooth_ext(solution, residual, inverse_diag, mu, lam, steps):
    midpoint = 0.5 * (HIGH_BOUND + LOW_BOUND)
    halfwidth = 0.5 * (HIGH_BOUND - LOW_BOUND)
    sharpness = midpoint / halfwidth
    weight_old = 1.0 / sharpness

    def extent(array):
        return (
            (array.shape[-3] - solution.shape[-3]) // 2,
            (array.shape[-2] - solution.shape[-2]) // 2,
        )

    def fit(array, like):
        ax, ay = extent(array)
        bx, by = extent(like)
        return crop_xy(array, ax - bx, ay - by)

    direction = fit(inverse_diag, residual) * residual / midpoint
    solution = solution + fit(direction, solution)
    coef_like = jnp.zeros(residual.shape[-3:], residual.dtype)
    residual = crop(residual, 1) - apply_ext(direction, fit(mu, coef_like), fit(lam, coef_like), 1.0)
    for _ in range(steps - 1):
        weight_new = 1.0 / (2.0 * sharpness - weight_old)
        direction = weight_new * weight_old * crop(direction, 1) + 2.0 * weight_new / halfwidth * (
            fit(inverse_diag, residual) * residual
        )
        solution = solution + fit(direction, solution)
        coef_like = jnp.zeros(residual.shape[-3:], residual.dtype)
        residual = crop(residual, 1) - apply_ext(
            direction, fit(mu, coef_like), fit(lam, coef_like), 1.0
        )
        weight_old = weight_new
    return (solution, residual)


def pair_matrix(coarse_z):
    fine = jnp.arange(2 * coarse_z) // 2
    return (fine[None, :] == jnp.arange(coarse_z)[:, None]).astype(jnp.float32)


def upsample_z(array, pairs):
    return jnp.einsum("...k,kj->...j", array, pairs, precision=lax.Precision.HIGHEST)


def restrict_z(array, pairs):
    return jnp.einsum("...j,kj->...k", array, pairs, precision=lax.Precision.HIGHEST)


def shards_body(rhs_field, shear_modulus, lame_lambda, group_start):
    width_x = rhs_field.shape[1]
    width_y = rhs_field.shape[2]
    width_z = rhs_field.shape[3]
    depth = SWEEPS
    gy = lax.axis_index("gy")
    count_y = lax.axis_size("gy")

    coarse_x = width_x // 2
    coarse_y = width_y // 2
    coarse_z = width_z // 2
    fine_reach = depth + 1
    res_rows = COARSE_SWEEPS + (depth + 2) // 2
    coef_rows = res_rows + 2
    deep_y = 2 * coef_rows

    stacked = jnp.concatenate([rhs_field, shear_modulus[None], lame_lambda[None]], axis=0)
    stacked = halo_x(stacked, depth + 1)
    stacked = halo_y(stacked, deep_y)
    mu_ext = stacked[3]
    lam_ext = stacked[4]
    rhs_ext = crop(stacked[0:3], 1)
    inside = inside_mask(width_x, width_y, depth, deep_y - 1)
    inverse_diag = jnp.where(inside[None], 1.0 / diagonal_ext(mu_ext, lam_ext, 1.0), 0.0)

    solution, residual_deep = smooth_ext(
        jnp.zeros_like(rhs_field), rhs_ext, inverse_diag, mu_ext, lam_ext, SWEEPS
    )
    deep_r = (residual_deep.shape[2] - width_y) // 2
    residual_y = crop_xy(residual_deep, 0, deep_r - fine_reach)
    pairs = pair_matrix(coarse_z)
    res_win = restrict_z(crop_xy(residual_deep, 0, deep_r - 2 * res_rows), pairs)
    res_win = res_win.reshape(3, coarse_x, 2, coarse_y + 2 * res_rows, 2, coarse_z).sum(axis=(2, 4))
    fine_coef = crop_xy(jnp.stack([mu_ext, lam_ext]), depth + 1, deep_y - 2 * coef_rows)
    coef_win = restrict_z(fine_coef, pairs)
    coef_win = coef_win.reshape(2, coarse_x, 2, coarse_y + 2 * coef_rows, 2, coarse_z)
    coef_win = coef_win.sum(axis=(2, 4)) / 8.0
    coarse_res = res_win[:, :, res_rows : res_rows + coarse_y]
    starts = group_start[0]
    members = same_group(starts)
    cells_dev = coarse_x * coarse_y * coarse_z

    sums = coarse_res.sum(axis=(1, 2, 3))
    slots = jnp.where(jnp.arange(count_y)[:, None] == gy, sums[None, :], 0.0)
    all_sums = lax.psum(slots, "gy")

    def blocks(array, rows):
        gap = jnp.zeros(array.shape[:2] + (coarse_y - rows,) + array.shape[3:], array.dtype)
        low = jnp.concatenate([gap, array[:, :, :rows]], axis=2)
        own = array[:, :, rows : rows + coarse_y]
        high = jnp.concatenate([array[:, :, rows + coarse_y :], gap], axis=2)
        return jnp.stack([low, own, high], axis=1)

    window = jnp.concatenate([blocks(res_win, res_rows), blocks(coef_win, coef_rows)], axis=0)
    next_start = lax.dynamic_index_in_dim(starts, jnp.minimum(gy + 1, count_y - 1), 0, keepdims=False)
    own_start = lax.dynamic_index_in_dim(starts, gy, 0, keepdims=False)
    window_starts = jnp.stack([jnp.zeros_like(own_start), own_start, next_start])
    coef_pad = pad_groups(window[3:5], window_starts)
    coarse_diag = diagonal(coef_pad[0], coef_pad[1], 4.0)
    owners = gy - 1 + jnp.arange(3)
    valid = (owners >= 0) & (owners < count_y)
    usable = valid[None, :, None, None, None] & (coarse_diag > 0.0)
    coarse_inverse = jnp.where(usable, 1.0 / coarse_diag, 0.0)

    def coarse_apply(field):
        return operate(pad_groups(field, window_starts), coef_pad[0], coef_pad[1], 4.0)

    window_res = window[0:3]
    smoothed, _ = smooth(
        jnp.zeros_like(window_res), window_res, coarse_inverse, coarse_apply, COARSE_SWEEPS
    )
    correction = jnp.moveaxis(smoothed, 1, 2).reshape(3, coarse_x, 3 * coarse_y, coarse_z)
    reach_c = (depth + 2) // 2
    corr_y = correction[:, :, coarse_y - reach_c : 2 * coarse_y + reach_c, :]
    corr_z = upsample_z(corr_y, pairs)
    fine_corr = jnp.broadcast_to(
        corr_z[:, :, None, :, None, :],
        (3, coarse_x, 2, corr_y.shape[2], 2, width_z),
    ).reshape(3, width_x, 2 * corr_y.shape[2], width_z)
    fine_depth = 2 * reach_c
    fine_corr = fine_corr[:, :, fine_depth - fine_reach : fine_corr.shape[2] - (fine_depth - fine_reach), :]
    fine_corr = halo_x(fine_corr, fine_reach)
    residual_ext = crop_xy(halo_x(residual_y, depth), 0, 1)

    totals = jnp.sum(members[:, :, None] * all_sums[None, :, :], axis=1)
    group_cells = jnp.sum(members, axis=1) * cells_dev
    group_shift = totals / (SHIFT_SCALE * group_cells[:, None])
    window_shift = jnp.take(group_shift, jnp.clip(owners, 0, count_y - 1), axis=0)
    window_shift = jnp.where(valid[:, None], window_shift, 0.0)
    count_x = lax.axis_size("gx")
    side = reach_c
    lows, highs = [], []
    for dx in range(side, 0, -1):
        lows.append(lax.ppermute(window_shift, "gx", [(i, i + dx) for i in range(count_x - dx)]))
        highs.append(lax.ppermute(window_shift, "gx", [(i + dx, i) for i in range(count_x - dx)]))
    block_shift = jnp.stack(lows + [window_shift] + highs[::-1])
    block_shift = jnp.repeat(jnp.moveaxis(block_shift, 2, 0), 2, axis=1)
    block_shift = block_shift[:, 2 * side - fine_reach : block_shift.shape[1] - (2 * side - fine_reach)]
    rows = jnp.array([fine_reach, width_y, fine_reach])
    block_shift = jnp.repeat(block_shift, rows, axis=2, total_repeat_length=width_y + 2 * fine_reach)
    fine_corr = fine_corr + block_shift[:, :, :, None]

    solution = solution + crop(fine_corr, fine_reach)
    coef_cut = (mu_ext.shape[-2] - fine_corr.shape[-2]) // 2
    residual_ext = residual_ext - apply_ext(
        fine_corr, crop_xy(mu_ext, 0, coef_cut), crop_xy(lam_ext, 0, coef_cut), 1.0
    )
    solution, residual = smooth_ext(
        solution, residual_ext, inverse_diag, mu_ext, lam_ext, SWEEPS
    )
    return (solution, residual)


def solution(mesh):
    return jax.shard_map(
        shards_body,
        mesh=mesh,
        in_specs=(
            P(None, "gx", "gy", None),
            P("gx", "gy", None),
            P("gx", "gy", None),
            P("gx", None),
        ),
        out_specs=(P(None, "gx", "gy", None), P(None, "gx", "gy", None)),
        check_vma=False,
    )
```

```python
import jax
import jax.numpy as jnp
from jax import lax
from jax.sharding import PartitionSpec as P

SWEEPS = 3
COARSE_SWEEPS = 4


LOW_BOUND = 0.5
HIGH_BOUND = 6.0
SHIFT_SCALE = 48.0
UNITS = ((1, 0, 0), (0, 1, 0), (0, 0, 1))


def shifted(array, step_x, step_y, step_z):
    size_x = array.shape[-3] - 2
    size_y = array.shape[-2] - 2
    size_z = array.shape[-1] - 2
    return array[
        ...,
        1 + step_x : 1 + step_x + size_x,
        1 + step_y : 1 + step_y + size_y,
        1 + step_z : 1 + step_z + size_z,
    ]


def diagonal(mu_pad, lam_pad, scale):
    mu_centre = shifted(mu_pad, 0, 0, 0)
    lam_centre = shifted(lam_pad, 0, 0, 0)
    faces = 0.0
    for unit in UNITS:
        backward = tuple((-value for value in unit))
        faces = (
            faces
            + 0.5 * (mu_centre + shifted(mu_pad, *unit))
            + 0.5 * (mu_centre + shifted(mu_pad, *backward))
        )
    results = []
    for unit in UNITS:
        backward = tuple((-value for value in unit))
        results.append(scale * (faces + lam_centre + shifted(lam_pad, *backward)))
    return jnp.stack(results)


def operate(field_pad, mu_pad, lam_pad, scale):
    mu_centre = shifted(mu_pad, 0, 0, 0)
    lam_centre = shifted(lam_pad, 0, 0, 0)
    components = [field_pad[0], field_pad[1], field_pad[2]]
    centres = [shifted(value, 0, 0, 0) for value in components]
    laplace = [0.0, 0.0, 0.0]
    for unit in UNITS:
        backward = tuple((-value for value in unit))
        face_up = 0.5 * (mu_centre + shifted(mu_pad, *unit))
        face_down = 0.5 * (mu_centre + shifted(mu_pad, *backward))
        for comp_id in range(3):
            laplace[comp_id] = (
                laplace[comp_id]
                + face_up * (shifted(components[comp_id], *unit) - centres[comp_id])
                - face_down * (centres[comp_id] - shifted(components[comp_id], *backward))
            )

    def spread(offset):
        total = 0.0
        for comp_id in range(3):
            ahead = tuple((offset[axis_id] + UNITS[comp_id][axis_id] for axis_id in range(3)))
            total = total + (
                shifted(components[comp_id], *ahead) - shifted(components[comp_id], *offset)
            )
        return total

    stress_here = lam_centre * spread((0, 0, 0))
    results = []
    for comp_id in range(3):
        backward = tuple((-value for value in UNITS[comp_id]))
        grad_term = stress_here - shifted(lam_pad, *backward) * spread(backward)
        results.append(scale * (-laplace[comp_id] - grad_term))
    return jnp.stack(results)


def smooth(solution, residual, inverse_diag, apply_fn, steps):
    midpoint = 0.5 * (HIGH_BOUND + LOW_BOUND)
    halfwidth = 0.5 * (HIGH_BOUND - LOW_BOUND)
    sharpness = midpoint / halfwidth
    weight_old = 1.0 / sharpness
    direction = inverse_diag * residual / midpoint
    solution = solution + direction
    residual = residual - apply_fn(direction)
    for step_id in range(steps - 1):
        weight_new = 1.0 / (2.0 * sharpness - weight_old)
        direction = weight_new * weight_old * direction + 2.0 * weight_new / halfwidth * (
            inverse_diag * residual
        )
        solution = solution + direction
        residual = residual - apply_fn(direction)
        weight_old = weight_new
    return (solution, residual)


def pad_groups(array, starts):
    cont = jnp.where(starts[..., 1:] == 0, 1.0, 0.0)
    closed = jnp.zeros_like(cont[..., :1])
    lower = jnp.concatenate([closed, cont], axis=-1)[..., None, None, None]
    upper = jnp.concatenate([cont, closed], axis=-1)[..., None, None, None]
    below = (
        jnp.concatenate(
            [jnp.zeros_like(array[..., :1, :, :1, :]), array[..., :-1, :, -1:, :]], axis=-4
        )
        * lower
    )
    above = (
        jnp.concatenate(
            [array[..., 1:, :, :1, :], jnp.zeros_like(array[..., :1, :, :1, :])], axis=-4
        )
        * upper
    )
    joined = jnp.concatenate([below, array, above], axis=-2)
    widths = [(0, 0)] * (joined.ndim - 3) + [(1, 1), (0, 0), (1, 1)]
    return jnp.pad(joined, widths)


def same_group(starts):
    count = starts.shape[-1]
    marks = jnp.where(jnp.arange(count, dtype=jnp.int32) > 0, starts, 0)
    labels = jnp.cumsum(marks, axis=-1)
    return jnp.where(labels[..., :, None] == labels[..., None, :], 1.0, 0.0).astype(jnp.float32)


def crop_xy(array, cut_x, cut_y):
    size_x = array.shape[-3]
    size_y = array.shape[-2]
    return array[..., cut_x : size_x - cut_x, cut_y : size_y - cut_y, :]


def crop(array, cut):
    if cut == 0:
        return array
    return array[..., cut:-cut, cut:-cut, :]


def shifted_ext(array, step_x, step_y, step_z):
    size_x = array.shape[-3] - 2
    size_y = array.shape[-2] - 2
    inner = array[..., 1 + step_x : 1 + step_x + size_x, 1 + step_y : 1 + step_y + size_y, :]
    if step_z == 0:
        return inner
    zero = jnp.zeros_like(inner[..., :1])
    if step_z > 0:
        return jnp.concatenate([inner[..., 1:], zero], axis=-1)
    return jnp.concatenate([zero, inner[..., :-1]], axis=-1)


def diagonal_ext(mu_pad, lam_pad, scale):
    mu_centre = shifted_ext(mu_pad, 0, 0, 0)
    lam_centre = shifted_ext(lam_pad, 0, 0, 0)
    faces = 0.0
    for unit in UNITS:
        backward = tuple((-value for value in unit))
        faces = (
            faces
            + 0.5 * (mu_centre + shifted_ext(mu_pad, *unit))
            + 0.5 * (mu_centre + shifted_ext(mu_pad, *backward))
        )
    results = []
    for unit in UNITS:
        backward = tuple((-value for value in unit))
        results.append(scale * (faces + lam_centre + shifted_ext(lam_pad, *backward)))
    return jnp.stack(results)


def apply_ext(field_pad, mu_pad, lam_pad, scale):
    mu_centre = shifted_ext(mu_pad, 0, 0, 0)
    lam_centre = shifted_ext(lam_pad, 0, 0, 0)
    components = [field_pad[0], field_pad[1], field_pad[2]]
    centres = [shifted_ext(value, 0, 0, 0) for value in components]
    laplace = [0.0, 0.0, 0.0]
    for unit in UNITS:
        backward = tuple((-value for value in unit))
        face_up = 0.5 * (mu_centre + shifted_ext(mu_pad, *unit))
        face_down = 0.5 * (mu_centre + shifted_ext(mu_pad, *backward))
        for comp_id in range(3):
            laplace[comp_id] = (
                laplace[comp_id]
                + face_up * (shifted_ext(components[comp_id], *unit) - centres[comp_id])
                - face_down * (centres[comp_id] - shifted_ext(components[comp_id], *backward))
            )

    def spread(offset):
        total = 0.0
        for comp_id in range(3):
            ahead = tuple((offset[axis_id] + UNITS[comp_id][axis_id] for axis_id in range(3)))
            total = total + (
                shifted_ext(components[comp_id], *ahead)
                - shifted_ext(components[comp_id], *offset)
            )
        return total

    stress_here = lam_centre * spread((0, 0, 0))
    results = []
    for comp_id in range(3):
        backward = tuple((-value for value in UNITS[comp_id]))
        grad_term = stress_here - shifted_ext(lam_pad, *backward) * spread(backward)
        results.append(scale * (-laplace[comp_id] - grad_term))
    return jnp.stack(results)


def halo_x(array, depth):
    count = lax.axis_size("gx")
    width = array.shape[-3]
    reach = (depth + width - 1) // width
    lows, highs = [], []
    for dx in range(reach, 0, -1):
        need = min(width, depth - (dx - 1) * width)
        forward = [(i, i + dx) for i in range(count - dx)]
        backward = [(i + dx, i) for i in range(count - dx)]
        lows.append(lax.ppermute(array[..., width - need :, :, :], "gx", forward))
        highs.append(lax.ppermute(array[..., :need, :, :], "gx", backward))
    return jnp.concatenate(lows + [array] + highs[::-1], axis=-3)


def halo_y(array, depth):
    count = lax.axis_size("gy")
    forward = [(i, i + 1) for i in range(count - 1)]
    backward = [(i + 1, i) for i in range(count - 1)]
    low = lax.ppermute(array[..., -depth:, :], "gy", forward)
    high = lax.ppermute(array[..., :depth, :], "gy", backward)
    return jnp.concatenate([low, array, high], axis=-2)


def inside_mask(width_x, width_y, depth_x, depth_y):
    gx = lax.axis_index("gx")
    gy = lax.axis_index("gy")
    total_x = width_x * lax.axis_size("gx")
    total_y = width_y * lax.axis_size("gy")
    xs = gx * width_x + jnp.arange(width_x + 2 * depth_x) - depth_x
    ys = gy * width_y + jnp.arange(width_y + 2 * depth_y) - depth_y
    ok_x = (xs >= 0) & (xs < total_x)
    ok_y = (ys >= 0) & (ys < total_y)
    return (ok_x[:, None] & ok_y[None, :])[:, :, None]


def smooth_ext(solution, residual, inverse_diag, mu, lam, steps):
    midpoint = 0.5 * (HIGH_BOUND + LOW_BOUND)
    halfwidth = 0.5 * (HIGH_BOUND - LOW_BOUND)
    sharpness = midpoint / halfwidth
    weight_old = 1.0 / sharpness

    def extent(array):
        return (
            (array.shape[-3] - solution.shape[-3]) // 2,
            (array.shape[-2] - solution.shape[-2]) // 2,
        )

    def fit(array, like):
        ax, ay = extent(array)
        bx, by = extent(like)
        return crop_xy(array, ax - bx, ay - by)

    direction = fit(inverse_diag, residual) * residual / midpoint
    solution = solution + fit(direction, solution)
    coef_like = jnp.zeros(residual.shape[-3:], residual.dtype)
    residual = crop(residual, 1) - apply_ext(direction, fit(mu, coef_like), fit(lam, coef_like), 1.0)
    for step_id in range(steps - 1):
        weight_new = 1.0 / (2.0 * sharpness - weight_old)
        direction = weight_new * weight_old * crop(direction, 1) + 2.0 * weight_new / halfwidth * (
            fit(inverse_diag, residual) * residual
        )
        solution = solution + fit(direction, solution)
        coef_like = jnp.zeros(residual.shape[-3:], residual.dtype)
        residual = crop(residual, 1) - apply_ext(
            direction, fit(mu, coef_like), fit(lam, coef_like), 1.0
        )
        weight_old = weight_new
    return (solution, residual)


def pair_matrix(coarse_z):
    fine = jnp.arange(2 * coarse_z) // 2
    return (fine[None, :] == jnp.arange(coarse_z)[:, None]).astype(jnp.float32)


def upsample_z(array, pairs):
    return jnp.einsum("...k,kj->...j", array, pairs, precision=lax.Precision.HIGHEST)


def restrict_z(array, pairs):
    return jnp.einsum("...j,kj->...k", array, pairs, precision=lax.Precision.HIGHEST)


def shards(rhs_field, shear_modulus, lame_lambda, group_start):
    width_x = rhs_field.shape[1]
    width_y = rhs_field.shape[2]
    width_z = rhs_field.shape[3]
    depth = SWEEPS
    gy = lax.axis_index("gy")
    count_y = lax.axis_size("gy")

    coarse_x = width_x // 2
    coarse_y = width_y // 2
    coarse_z = width_z // 2
    fine_reach = depth + 1
    res_rows = COARSE_SWEEPS + (depth + 2) // 2
    coef_rows = res_rows + 2
    deep_y = 2 * coef_rows

    stacked = jnp.concatenate([rhs_field, shear_modulus[None], lame_lambda[None]], axis=0)
    stacked = halo_x(stacked, depth + 1)
    stacked = halo_y(stacked, deep_y)
    mu_ext = stacked[3]
    lam_ext = stacked[4]
    rhs_ext = crop(stacked[0:3], 1)
    inside = inside_mask(width_x, width_y, depth, deep_y - 1)
    inverse_diag = jnp.where(inside[None], 1.0 / diagonal_ext(mu_ext, lam_ext, 1.0), 0.0)

    solution, residual_deep = smooth_ext(
        jnp.zeros_like(rhs_field), rhs_ext, inverse_diag, mu_ext, lam_ext, SWEEPS
    )
    deep_r = (residual_deep.shape[2] - width_y) // 2
    residual_y = crop_xy(residual_deep, 0, deep_r - fine_reach)
    pairs = pair_matrix(coarse_z)
    res_win = restrict_z(crop_xy(residual_deep, 0, deep_r - 2 * res_rows), pairs)
    res_win = res_win.reshape(3, coarse_x, 2, coarse_y + 2 * res_rows, 2, coarse_z).sum(axis=(2, 4))
    fine_coef = crop_xy(jnp.stack([mu_ext, lam_ext]), depth + 1, deep_y - 2 * coef_rows)
    coef_win = restrict_z(fine_coef, pairs)
    coef_win = coef_win.reshape(2, coarse_x, 2, coarse_y + 2 * coef_rows, 2, coarse_z)
    coef_win = coef_win.sum(axis=(2, 4)) / 8.0
    coarse_res = res_win[:, :, res_rows : res_rows + coarse_y]
    starts = group_start[0]
    members = same_group(starts)
    cells_dev = coarse_x * coarse_y * coarse_z

    sums = coarse_res.sum(axis=(1, 2, 3))
    slots = jnp.where(jnp.arange(count_y)[:, None] == gy, sums[None, :], 0.0)
    all_sums = lax.psum(slots, "gy")

    def blocks(array, rows):
        gap = jnp.zeros(array.shape[:2] + (coarse_y - rows,) + array.shape[3:], array.dtype)
        low = jnp.concatenate([gap, array[:, :, :rows]], axis=2)
        own = array[:, :, rows : rows + coarse_y]
        high = jnp.concatenate([array[:, :, rows + coarse_y :], gap], axis=2)
        return jnp.stack([low, own, high], axis=1)

    window = jnp.concatenate([blocks(res_win, res_rows), blocks(coef_win, coef_rows)], axis=0)
    next_start = lax.dynamic_index_in_dim(starts, jnp.minimum(gy + 1, count_y - 1), 0, keepdims=False)
    own_start = lax.dynamic_index_in_dim(starts, gy, 0, keepdims=False)
    window_starts = jnp.stack([jnp.zeros_like(own_start), own_start, next_start])
    coef_pad = pad_groups(window[3:5], window_starts)
    coarse_diag = diagonal(coef_pad[0], coef_pad[1], 4.0)
    owners = gy - 1 + jnp.arange(3)
    valid = (owners >= 0) & (owners < count_y)
    usable = valid[None, :, None, None, None] & (coarse_diag > 0.0)
    coarse_inverse = jnp.where(usable, 1.0 / coarse_diag, 0.0)

    def coarse_apply(field):
        return operate(pad_groups(field, window_starts), coef_pad[0], coef_pad[1], 4.0)

    window_res = window[0:3]
    smoothed, coarse_left = smooth(
        jnp.zeros_like(window_res), window_res, coarse_inverse, coarse_apply, COARSE_SWEEPS
    )
    totals = jnp.sum(members[:, :, None] * all_sums[None, :, :], axis=1)
    group_cells = jnp.sum(members, axis=1) * cells_dev
    group_shift = totals / (SHIFT_SCALE * group_cells[:, None])
    window_shift = jnp.take(group_shift, jnp.clip(owners, 0, count_y - 1), axis=0)
    window_shift = jnp.where(valid[:, None], window_shift, 0.0)
    correction = smoothed + window_shift.T[:, :, None, None, None]
    correction = jnp.moveaxis(correction, 1, 2).reshape(3, coarse_x, 3 * coarse_y, coarse_z)
    reach_c = (depth + 2) // 2
    corr_y = correction[:, :, coarse_y - reach_c : 2 * coarse_y + reach_c, :]
    corr_z = upsample_z(corr_y, pairs)
    corr_rows = corr_z.shape[2]
    slab = 8 * ((corr_rows + 15) // 16)
    corr_pad = jnp.pad(corr_z, ((0, 0), (0, 0), (0, 2 * slab - corr_rows), (0, 0)))
    count_x = lax.axis_size("gx")
    edge_rows = residual_y.shape[2]
    lows_r, highs_r, lows_c, highs_c = [], [], [], []
    for dx in range(reach_c, 0, -1):
        forward = [(i, i + dx) for i in range(count_x - dx)]
        backward = [(i + dx, i) for i in range(count_x - dx)]
        need = min(width_x, depth - (dx - 1) * width_x)
        if need == width_x:
            corr_part = corr_pad.reshape(3, width_x, slab, width_z)
        else:
            corr_part = corr_pad
        send_low = jnp.concatenate([residual_y[:, width_x - need :], corr_part[:, : need]], axis=2)
        send_high = jnp.concatenate([residual_y[:, :need], corr_part[:, :need]], axis=2)
        got_low = lax.ppermute(send_low, "gx", forward)
        got_high = lax.ppermute(send_high, "gx", backward)
        lows_r.append(got_low[:, :, :edge_rows])
        highs_r.append(got_high[:, :, :edge_rows])
        lows_c.append(got_low[:, :, edge_rows:].reshape(3, 1, -1, width_z)[:, :, :corr_rows])
        highs_c.append(got_high[:, :, edge_rows:].reshape(3, 1, -1, width_z)[:, :, :corr_rows])
    residual_ext = crop_xy(jnp.concatenate(lows_r + [residual_y] + highs_r[::-1], axis=1), 0, 1)
    corr_cols = jnp.concatenate(lows_c + [corr_z] + highs_c[::-1], axis=1)
    fine_corr = jnp.broadcast_to(
        corr_cols[:, :, None, :, None, :],
        (3, corr_cols.shape[1], 2, corr_rows, 2, width_z),
    ).reshape(3, 2 * corr_cols.shape[1], 2 * corr_rows, width_z)
    fine_depth = 2 * reach_c
    fine_corr = crop(fine_corr, fine_depth - fine_reach)
    solution = solution + crop(fine_corr, fine_reach)
    coef_cut = (mu_ext.shape[-2] - fine_corr.shape[-2]) // 2
    residual_ext = residual_ext - apply_ext(
        fine_corr, crop_xy(mu_ext, 0, coef_cut), crop_xy(lam_ext, 0, coef_cut), 1.0
    )
    solution, residual = smooth_ext(
        solution, residual_ext, inverse_diag, mu_ext, lam_ext, SWEEPS
    )
    return (solution, residual)


def solution(mesh):
    return jax.shard_map(
        shards,
        mesh=mesh,
        in_specs=(
            P(None, "gx", "gy", None),
            P("gx", "gy", None),
            P("gx", "gy", None),
            P("gx", None),
        ),
        out_specs=(P(None, "gx", "gy", None), P(None, "gx", "gy", None)),
        check_vma=False,
    )
```

```python
import jax
import jax.numpy as jnp
from jax import lax
from jax.sharding import PartitionSpec as P

SWEEPS = 3
COARSE_SWEEPS = 4


LOW_BOUND = 0.5
HIGH_BOUND = 6.0
SHIFT_SCALE = 48.0
UNITS = ((1, 0, 0), (0, 1, 0), (0, 0, 1))


def shifted(array, step_x, step_y, step_z):
    size_x = array.shape[-3] - 2
    size_y = array.shape[-2] - 2
    size_z = array.shape[-1] - 2
    return array[
        ...,
        1 + step_x : 1 + step_x + size_x,
        1 + step_y : 1 + step_y + size_y,
        1 + step_z : 1 + step_z + size_z,
    ]


def diagonal(mu_pad, lam_pad, scale):
    mu_centre = shifted(mu_pad, 0, 0, 0)
    lam_centre = shifted(lam_pad, 0, 0, 0)
    faces = 0.0
    for unit in UNITS:
        backward = tuple((-value for value in unit))
        faces = (
            faces
            + 0.5 * (mu_centre + shifted(mu_pad, *unit))
            + 0.5 * (mu_centre + shifted(mu_pad, *backward))
        )
    results = []
    for unit in UNITS:
        backward = tuple((-value for value in unit))
        results.append(scale * (faces + lam_centre + shifted(lam_pad, *backward)))
    return jnp.stack(results)


def operate(field_pad, mu_pad, lam_pad, scale):
    mu_centre = shifted(mu_pad, 0, 0, 0)
    lam_centre = shifted(lam_pad, 0, 0, 0)
    components = [field_pad[0], field_pad[1], field_pad[2]]
    centres = [shifted(value, 0, 0, 0) for value in components]
    laplace = [0.0, 0.0, 0.0]
    for unit in UNITS:
        backward = tuple((-value for value in unit))
        face_up = 0.5 * (mu_centre + shifted(mu_pad, *unit))
        face_down = 0.5 * (mu_centre + shifted(mu_pad, *backward))
        for comp_id in range(3):
            laplace[comp_id] = (
                laplace[comp_id]
                + face_up * (shifted(components[comp_id], *unit) - centres[comp_id])
                - face_down * (centres[comp_id] - shifted(components[comp_id], *backward))
            )

    def spread(offset):
        total = 0.0
        for comp_id in range(3):
            ahead = tuple((offset[axis_id] + UNITS[comp_id][axis_id] for axis_id in range(3)))
            total = total + (
                shifted(components[comp_id], *ahead) - shifted(components[comp_id], *offset)
            )
        return total

    stress_here = lam_centre * spread((0, 0, 0))
    results = []
    for comp_id in range(3):
        backward = tuple((-value for value in UNITS[comp_id]))
        grad_term = stress_here - shifted(lam_pad, *backward) * spread(backward)
        results.append(scale * (-laplace[comp_id] - grad_term))
    return jnp.stack(results)


def smooth(solution, residual, inverse_diag, apply_fn, steps):
    midpoint = 0.5 * (HIGH_BOUND + LOW_BOUND)
    halfwidth = 0.5 * (HIGH_BOUND - LOW_BOUND)
    sharpness = midpoint / halfwidth
    weight_old = 1.0 / sharpness
    direction = inverse_diag * residual / midpoint
    solution = solution + direction
    residual = residual - apply_fn(direction)
    for step_id in range(steps - 1):
        weight_new = 1.0 / (2.0 * sharpness - weight_old)
        direction = weight_new * weight_old * direction + 2.0 * weight_new / halfwidth * (
            inverse_diag * residual
        )
        solution = solution + direction
        residual = residual - apply_fn(direction)
        weight_old = weight_new
    return (solution, residual)


def pad_groups(array, starts):
    cont = jnp.where(starts[..., 1:] == 0, 1.0, 0.0)
    closed = jnp.zeros_like(cont[..., :1])
    lower = jnp.concatenate([closed, cont], axis=-1)[..., None, None, None]
    upper = jnp.concatenate([cont, closed], axis=-1)[..., None, None, None]
    below = (
        jnp.concatenate(
            [jnp.zeros_like(array[..., :1, :, :1, :]), array[..., :-1, :, -1:, :]], axis=-4
        )
        * lower
    )
    above = (
        jnp.concatenate(
            [array[..., 1:, :, :1, :], jnp.zeros_like(array[..., :1, :, :1, :])], axis=-4
        )
        * upper
    )
    joined = jnp.concatenate([below, array, above], axis=-2)
    widths = [(0, 0)] * (joined.ndim - 3) + [(1, 1), (0, 0), (1, 1)]
    return jnp.pad(joined, widths)


def same_group(starts):
    count = starts.shape[-1]
    marks = jnp.where(jnp.arange(count, dtype=jnp.int32) > 0, starts, 0)
    labels = jnp.cumsum(marks, axis=-1)
    return jnp.where(labels[..., :, None] == labels[..., None, :], 1.0, 0.0).astype(jnp.float32)


def crop_xy(array, cut_x, cut_y):
    size_x = array.shape[-3]
    size_y = array.shape[-2]
    return array[..., cut_x : size_x - cut_x, cut_y : size_y - cut_y, :]


def crop(array, cut):
    if cut == 0:
        return array
    return array[..., cut:-cut, cut:-cut, :]


def shifted_ext(array, step_x, step_y, step_z):
    size_x = array.shape[-3] - 2
    size_y = array.shape[-2] - 2
    inner = array[..., 1 + step_x : 1 + step_x + size_x, 1 + step_y : 1 + step_y + size_y, :]
    if step_z == 0:
        return inner
    zero = jnp.zeros_like(inner[..., :1])
    if step_z > 0:
        return jnp.concatenate([inner[..., 1:], zero], axis=-1)
    return jnp.concatenate([zero, inner[..., :-1]], axis=-1)


def diagonal_ext(mu_pad, lam_pad, scale):
    mu_centre = shifted_ext(mu_pad, 0, 0, 0)
    lam_centre = shifted_ext(lam_pad, 0, 0, 0)
    faces = 0.0
    for unit in UNITS:
        backward = tuple((-value for value in unit))
        faces = (
            faces
            + 0.5 * (mu_centre + shifted_ext(mu_pad, *unit))
            + 0.5 * (mu_centre + shifted_ext(mu_pad, *backward))
        )
    results = []
    for unit in UNITS:
        backward = tuple((-value for value in unit))
        results.append(scale * (faces + lam_centre + shifted_ext(lam_pad, *backward)))
    return jnp.stack(results)


def apply_ext(field_pad, mu_pad, lam_pad, scale):
    mu_centre = shifted_ext(mu_pad, 0, 0, 0)
    lam_centre = shifted_ext(lam_pad, 0, 0, 0)
    components = [field_pad[0], field_pad[1], field_pad[2]]
    centres = [shifted_ext(value, 0, 0, 0) for value in components]
    laplace = [0.0, 0.0, 0.0]
    for unit in UNITS:
        backward = tuple((-value for value in unit))
        face_up = 0.5 * (mu_centre + shifted_ext(mu_pad, *unit))
        face_down = 0.5 * (mu_centre + shifted_ext(mu_pad, *backward))
        for comp_id in range(3):
            laplace[comp_id] = (
                laplace[comp_id]
                + face_up * (shifted_ext(components[comp_id], *unit) - centres[comp_id])
                - face_down * (centres[comp_id] - shifted_ext(components[comp_id], *backward))
            )

    def spread(offset):
        total = 0.0
        for comp_id in range(3):
            ahead = tuple((offset[axis_id] + UNITS[comp_id][axis_id] for axis_id in range(3)))
            total = total + (
                shifted_ext(components[comp_id], *ahead)
                - shifted_ext(components[comp_id], *offset)
            )
        return total

    stress_here = lam_centre * spread((0, 0, 0))
    results = []
    for comp_id in range(3):
        backward = tuple((-value for value in UNITS[comp_id]))
        grad_term = stress_here - shifted_ext(lam_pad, *backward) * spread(backward)
        results.append(scale * (-laplace[comp_id] - grad_term))
    return jnp.stack(results)


def halo_x(array, depth):
    count = lax.axis_size("gx")
    width = array.shape[-3]
    reach = (depth + width - 1) // width
    lows, highs = [], []
    for dx in range(reach, 0, -1):
        need = min(width, depth - (dx - 1) * width)
        forward = [(i, i + dx) for i in range(count - dx)]
        backward = [(i + dx, i) for i in range(count - dx)]
        lows.append(lax.ppermute(array[..., width - need :, :, :], "gx", forward))
        highs.append(lax.ppermute(array[..., :need, :, :], "gx", backward))
    return jnp.concatenate(lows + [array] + highs[::-1], axis=-3)


def halo_y(array, depth):
    count = lax.axis_size("gy")
    forward = [(i, i + 1) for i in range(count - 1)]
    backward = [(i + 1, i) for i in range(count - 1)]
    low = lax.ppermute(array[..., -depth:, :], "gy", forward)
    high = lax.ppermute(array[..., :depth, :], "gy", backward)
    return jnp.concatenate([low, array, high], axis=-2)


def inside_mask(width_x, width_y, depth_x, depth_y):
    gx = lax.axis_index("gx")
    gy = lax.axis_index("gy")
    total_x = width_x * lax.axis_size("gx")
    total_y = width_y * lax.axis_size("gy")
    xs = gx * width_x + jnp.arange(width_x + 2 * depth_x) - depth_x
    ys = gy * width_y + jnp.arange(width_y + 2 * depth_y) - depth_y
    ok_x = (xs >= 0) & (xs < total_x)
    ok_y = (ys >= 0) & (ys < total_y)
    return (ok_x[:, None] & ok_y[None, :])[:, :, None]


def smooth_ext(solution, residual, inverse_diag, mu, lam, steps):
    midpoint = 0.5 * (HIGH_BOUND + LOW_BOUND)
    halfwidth = 0.5 * (HIGH_BOUND - LOW_BOUND)
    sharpness = midpoint / halfwidth
    weight_old = 1.0 / sharpness

    def extent(array):
        return (
            (array.shape[-3] - solution.shape[-3]) // 2,
            (array.shape[-2] - solution.shape[-2]) // 2,
        )

    def fit(array, like):
        ax, ay = extent(array)
        bx, by = extent(like)
        return crop_xy(array, ax - bx, ay - by)

    direction = fit(inverse_diag, residual) * residual / midpoint
    solution = solution + fit(direction, solution)
    coef_like = jnp.zeros(residual.shape[-3:], residual.dtype)
    residual = crop(residual, 1) - apply_ext(direction, fit(mu, coef_like), fit(lam, coef_like), 1.0)
    for step_id in range(steps - 1):
        weight_new = 1.0 / (2.0 * sharpness - weight_old)
        direction = weight_new * weight_old * crop(direction, 1) + 2.0 * weight_new / halfwidth * (
            fit(inverse_diag, residual) * residual
        )
        solution = solution + fit(direction, solution)
        coef_like = jnp.zeros(residual.shape[-3:], residual.dtype)
        residual = crop(residual, 1) - apply_ext(
            direction, fit(mu, coef_like), fit(lam, coef_like), 1.0
        )
        weight_old = weight_new
    return (solution, residual)


def pair_matrix(coarse_z):
    fine = jnp.arange(2 * coarse_z) // 2
    return (fine[None, :] == jnp.arange(coarse_z)[:, None]).astype(jnp.float32)


def upsample_z(array, pairs):
    return jnp.einsum("...k,kj->...j", array, pairs, precision=lax.Precision.HIGHEST)


def restrict_z(array, pairs):
    return jnp.einsum("...j,kj->...k", array, pairs, precision=lax.Precision.HIGHEST)


def shards(rhs_field, shear_modulus, lame_lambda, group_start):
    width_x = rhs_field.shape[1]
    width_y = rhs_field.shape[2]
    width_z = rhs_field.shape[3]
    depth = SWEEPS
    gy = lax.axis_index("gy")
    count_y = lax.axis_size("gy")

    coarse_x = width_x // 2
    coarse_y = width_y // 2
    coarse_z = width_z // 2
    fine_reach = depth + 1
    res_rows = COARSE_SWEEPS + (depth + 2) // 2 - 1
    coef_rows = res_rows + 1
    deep_y = 2 * res_rows + depth + 1

    stacked = jnp.concatenate([rhs_field, shear_modulus[None], lame_lambda[None]], axis=0)
    stacked = halo_x(stacked, depth + 1)
    stacked = halo_y(stacked, deep_y)
    mu_ext = stacked[3]
    lam_ext = stacked[4]
    rhs_ext = crop(stacked[0:3], 1)
    inside = inside_mask(width_x, width_y, depth, deep_y - 1)
    inverse_diag = jnp.where(inside[None], 1.0 / diagonal_ext(mu_ext, lam_ext, 1.0), 0.0)

    solution, residual_deep = smooth_ext(
        jnp.zeros_like(rhs_field), rhs_ext, inverse_diag, mu_ext, lam_ext, SWEEPS
    )
    deep_r = (residual_deep.shape[2] - width_y) // 2
    residual_y = crop_xy(residual_deep, 0, deep_r - fine_reach)
    pairs = pair_matrix(coarse_z)
    res_win = restrict_z(crop_xy(residual_deep, 0, deep_r - 2 * res_rows), pairs)
    res_win = res_win.reshape(3, coarse_x, 2, coarse_y + 2 * res_rows, 2, coarse_z).sum(axis=(2, 4))
    fine_coef = crop_xy(jnp.stack([mu_ext, lam_ext]), depth + 1, deep_y - 2 * coef_rows)
    coef_win = restrict_z(fine_coef, pairs)
    coef_win = coef_win.reshape(2, coarse_x, 2, coarse_y + 2 * coef_rows, 2, coarse_z)
    coef_win = coef_win.sum(axis=(2, 4)) / 8.0
    coarse_res = res_win[:, :, res_rows : res_rows + coarse_y]
    starts = group_start[0]
    members = same_group(starts)
    cells_dev = coarse_x * coarse_y * coarse_z

    sums = coarse_res.sum(axis=(1, 2, 3))
    slots = jnp.where(jnp.arange(count_y)[:, None] == gy, sums[None, :], 0.0)
    all_sums = lax.psum(slots, "gy")

    def blocks(array, rows):
        gap = jnp.zeros(array.shape[:2] + (coarse_y - rows,) + array.shape[3:], array.dtype)
        low = jnp.concatenate([gap, array[:, :, :rows]], axis=2)
        own = array[:, :, rows : rows + coarse_y]
        high = jnp.concatenate([array[:, :, rows + coarse_y :], gap], axis=2)
        return jnp.stack([low, own, high], axis=1)

    window = jnp.concatenate([blocks(res_win, res_rows), blocks(coef_win, coef_rows)], axis=0)
    next_start = lax.dynamic_index_in_dim(starts, jnp.minimum(gy + 1, count_y - 1), 0, keepdims=False)
    own_start = lax.dynamic_index_in_dim(starts, gy, 0, keepdims=False)
    window_starts = jnp.stack([jnp.zeros_like(own_start), own_start, next_start])
    coef_pad = pad_groups(window[3:5], window_starts)
    coarse_diag = diagonal(coef_pad[0], coef_pad[1], 4.0)
    owners = gy - 1 + jnp.arange(3)
    valid = (owners >= 0) & (owners < count_y)
    usable = valid[None, :, None, None, None] & (coarse_diag > 0.0)
    coarse_inverse = jnp.where(usable, 1.0 / coarse_diag, 0.0)

    def coarse_apply(field):
        return operate(pad_groups(field, window_starts), coef_pad[0], coef_pad[1], 4.0)

    window_res = window[0:3]
    smoothed, coarse_left = smooth(
        jnp.zeros_like(window_res), window_res, coarse_inverse, coarse_apply, COARSE_SWEEPS
    )
    totals = jnp.sum(members[:, :, None] * all_sums[None, :, :], axis=1)
    group_cells = jnp.sum(members, axis=1) * cells_dev
    group_shift = totals / (SHIFT_SCALE * group_cells[:, None])
    window_shift = jnp.take(group_shift, jnp.clip(owners, 0, count_y - 1), axis=0)
    window_shift = jnp.where(valid[:, None], window_shift, 0.0)
    correction = smoothed + window_shift.T[:, :, None, None, None]
    correction = jnp.moveaxis(correction, 1, 2).reshape(3, coarse_x, 3 * coarse_y, coarse_z)
    reach_c = (depth + 2) // 2
    corr_y = correction[:, :, coarse_y - reach_c : 2 * coarse_y + reach_c, :]
    corr_z = upsample_z(corr_y, pairs)
    corr_rows = corr_z.shape[2]
    slab = 8 * ((corr_rows + 15) // 16)
    corr_pad = jnp.pad(corr_z, ((0, 0), (0, 0), (0, 2 * slab - corr_rows), (0, 0)))
    count_x = lax.axis_size("gx")
    edge_rows = residual_y.shape[2]
    lows_r, highs_r, lows_c, highs_c = [], [], [], []
    for dx in range(reach_c, 0, -1):
        forward = [(i, i + dx) for i in range(count_x - dx)]
        backward = [(i + dx, i) for i in range(count_x - dx)]
        need = min(width_x, depth - (dx - 1) * width_x)
        if need == width_x:
            corr_part = corr_pad.reshape(3, width_x, slab, width_z)
        else:
            corr_part = corr_pad
        send_low = jnp.concatenate([residual_y[:, width_x - need :], corr_part[:, : need]], axis=2)
        send_high = jnp.concatenate([residual_y[:, :need], corr_part[:, :need]], axis=2)
        got_low = lax.ppermute(send_low, "gx", forward)
        got_high = lax.ppermute(send_high, "gx", backward)
        lows_r.append(got_low[:, :, :edge_rows])
        highs_r.append(got_high[:, :, :edge_rows])
        lows_c.append(got_low[:, :, edge_rows:].reshape(3, 1, -1, width_z)[:, :, :corr_rows])
        highs_c.append(got_high[:, :, edge_rows:].reshape(3, 1, -1, width_z)[:, :, :corr_rows])
    residual_ext = crop_xy(jnp.concatenate(lows_r + [residual_y] + highs_r[::-1], axis=1), 0, 1)
    corr_cols = jnp.concatenate(lows_c + [corr_z] + highs_c[::-1], axis=1)
    fine_corr = jnp.broadcast_to(
        corr_cols[:, :, None, :, None, :],
        (3, corr_cols.shape[1], 2, corr_rows, 2, width_z),
    ).reshape(3, 2 * corr_cols.shape[1], 2 * corr_rows, width_z)
    fine_depth = 2 * reach_c
    fine_corr = crop(fine_corr, fine_depth - fine_reach)
    solution = solution + crop(fine_corr, fine_reach)
    coef_cut = (mu_ext.shape[-2] - fine_corr.shape[-2]) // 2
    residual_ext = residual_ext - apply_ext(
        fine_corr, crop_xy(mu_ext, 0, coef_cut), crop_xy(lam_ext, 0, coef_cut), 1.0
    )
    solution, residual = smooth_ext(
        solution, residual_ext, inverse_diag, mu_ext, lam_ext, SWEEPS
    )
    return (solution, residual)


def solution(mesh):
    return jax.shard_map(
        shards,
        mesh=mesh,
        in_specs=(
            P(None, "gx", "gy", None),
            P("gx", "gy", None),
            P("gx", "gy", None),
            P("gx", None),
        ),
        out_specs=(P(None, "gx", "gy", None), P(None, "gx", "gy", None)),
        check_vma=False,
    )
```

```python
import jax
import jax.numpy as jnp
from jax import lax
from jax.sharding import PartitionSpec as P

SWEEPS = 3
COARSE_SWEEPS = 4


LOW_BOUND = 0.5
HIGH_BOUND = 6.0
SHIFT_SCALE = 48.0
UNITS = ((1, 0, 0), (0, 1, 0), (0, 0, 1))


def shifted(array, step_x, step_y, step_z):
    size_x = array.shape[-3] - 2
    size_y = array.shape[-2] - 2
    size_z = array.shape[-1] - 2
    return array[
        ...,
        1 + step_x : 1 + step_x + size_x,
        1 + step_y : 1 + step_y + size_y,
        1 + step_z : 1 + step_z + size_z,
    ]


def diagonal(mu_pad, lam_pad, scale):
    mu_centre = shifted(mu_pad, 0, 0, 0)
    lam_centre = shifted(lam_pad, 0, 0, 0)
    faces = 0.0
    for unit in UNITS:
        backward = tuple((-value for value in unit))
        faces = (
            faces
            + 0.5 * (mu_centre + shifted(mu_pad, *unit))
            + 0.5 * (mu_centre + shifted(mu_pad, *backward))
        )
    results = []
    for unit in UNITS:
        backward = tuple((-value for value in unit))
        results.append(scale * (faces + lam_centre + shifted(lam_pad, *backward)))
    return jnp.stack(results)


def operate(field_pad, mu_pad, lam_pad, scale):
    mu_centre = shifted(mu_pad, 0, 0, 0)
    lam_centre = shifted(lam_pad, 0, 0, 0)
    components = [field_pad[0], field_pad[1], field_pad[2]]
    centres = [shifted(value, 0, 0, 0) for value in components]
    laplace = [0.0, 0.0, 0.0]
    for unit in UNITS:
        backward = tuple((-value for value in unit))
        face_up = 0.5 * (mu_centre + shifted(mu_pad, *unit))
        face_down = 0.5 * (mu_centre + shifted(mu_pad, *backward))
        for comp_id in range(3):
            laplace[comp_id] = (
                laplace[comp_id]
                + face_up * (shifted(components[comp_id], *unit) - centres[comp_id])
                - face_down * (centres[comp_id] - shifted(components[comp_id], *backward))
            )

    def spread(offset):
        total = 0.0
        for comp_id in range(3):
            ahead = tuple((offset[axis_id] + UNITS[comp_id][axis_id] for axis_id in range(3)))
            total = total + (
                shifted(components[comp_id], *ahead) - shifted(components[comp_id], *offset)
            )
        return total

    stress_here = lam_centre * spread((0, 0, 0))
    results = []
    for comp_id in range(3):
        backward = tuple((-value for value in UNITS[comp_id]))
        grad_term = stress_here - shifted(lam_pad, *backward) * spread(backward)
        results.append(scale * (-laplace[comp_id] - grad_term))
    return jnp.stack(results)


def smooth(solution, residual, inverse_diag, apply_fn, steps):
    midpoint = 0.5 * (HIGH_BOUND + LOW_BOUND)
    halfwidth = 0.5 * (HIGH_BOUND - LOW_BOUND)
    sharpness = midpoint / halfwidth
    weight_old = 1.0 / sharpness
    direction = inverse_diag * residual / midpoint
    solution = solution + direction
    residual = residual - apply_fn(direction)
    for step_id in range(steps - 1):
        weight_new = 1.0 / (2.0 * sharpness - weight_old)
        direction = weight_new * weight_old * direction + 2.0 * weight_new / halfwidth * (
            inverse_diag * residual
        )
        solution = solution + direction
        residual = residual - apply_fn(direction)
        weight_old = weight_new
    return (solution, residual)


def pad_groups(array, starts):
    cont = jnp.where(starts[..., 1:] == 0, 1.0, 0.0)
    closed = jnp.zeros_like(cont[..., :1])
    lower = jnp.concatenate([closed, cont], axis=-1)[..., None, None, None]
    upper = jnp.concatenate([cont, closed], axis=-1)[..., None, None, None]
    below = (
        jnp.concatenate(
            [jnp.zeros_like(array[..., :1, :, :1, :]), array[..., :-1, :, -1:, :]], axis=-4
        )
        * lower
    )
    above = (
        jnp.concatenate(
            [array[..., 1:, :, :1, :], jnp.zeros_like(array[..., :1, :, :1, :])], axis=-4
        )
        * upper
    )
    joined = jnp.concatenate([below, array, above], axis=-2)
    widths = [(0, 0)] * (joined.ndim - 3) + [(1, 1), (0, 0), (1, 1)]
    return jnp.pad(joined, widths)


def same_group(starts):
    count = starts.shape[-1]
    marks = jnp.where(jnp.arange(count, dtype=jnp.int32) > 0, starts, 0)
    labels = jnp.cumsum(marks, axis=-1)
    return jnp.where(labels[..., :, None] == labels[..., None, :], 1.0, 0.0).astype(jnp.float32)


def crop_xy(array, cut_x, cut_y):
    size_x = array.shape[-3]
    size_y = array.shape[-2]
    return array[..., cut_x : size_x - cut_x, cut_y : size_y - cut_y, :]


def crop(array, cut):
    if cut == 0:
        return array
    return array[..., cut:-cut, cut:-cut, :]


def shifted_ext(array, step_x, step_y, step_z):
    size_x = array.shape[-3] - 2
    size_y = array.shape[-2] - 2
    inner = array[..., 1 + step_x : 1 + step_x + size_x, 1 + step_y : 1 + step_y + size_y, :]
    if step_z == 0:
        return inner
    zero = jnp.zeros_like(inner[..., :1])
    if step_z > 0:
        return jnp.concatenate([inner[..., 1:], zero], axis=-1)
    return jnp.concatenate([zero, inner[..., :-1]], axis=-1)


def diagonal_ext(mu_pad, lam_pad, scale):
    mu_centre = shifted_ext(mu_pad, 0, 0, 0)
    lam_centre = shifted_ext(lam_pad, 0, 0, 0)
    faces = 0.0
    for unit in UNITS:
        backward = tuple((-value for value in unit))
        faces = (
            faces
            + 0.5 * (mu_centre + shifted_ext(mu_pad, *unit))
            + 0.5 * (mu_centre + shifted_ext(mu_pad, *backward))
        )
    results = []
    for unit in UNITS:
        backward = tuple((-value for value in unit))
        results.append(scale * (faces + lam_centre + shifted_ext(lam_pad, *backward)))
    return jnp.stack(results)


def apply_ext(field_pad, mu_pad, lam_pad, scale):
    mu_centre = shifted_ext(mu_pad, 0, 0, 0)
    lam_centre = shifted_ext(lam_pad, 0, 0, 0)
    components = [field_pad[0], field_pad[1], field_pad[2]]
    centres = [shifted_ext(value, 0, 0, 0) for value in components]
    laplace = [0.0, 0.0, 0.0]
    for unit in UNITS:
        backward = tuple((-value for value in unit))
        face_up = 0.5 * (mu_centre + shifted_ext(mu_pad, *unit))
        face_down = 0.5 * (mu_centre + shifted_ext(mu_pad, *backward))
        for comp_id in range(3):
            laplace[comp_id] = (
                laplace[comp_id]
                + face_up * (shifted_ext(components[comp_id], *unit) - centres[comp_id])
                - face_down * (centres[comp_id] - shifted_ext(components[comp_id], *backward))
            )

    def spread(offset):
        total = 0.0
        for comp_id in range(3):
            ahead = tuple((offset[axis_id] + UNITS[comp_id][axis_id] for axis_id in range(3)))
            total = total + (
                shifted_ext(components[comp_id], *ahead)
                - shifted_ext(components[comp_id], *offset)
            )
        return total

    stress_here = lam_centre * spread((0, 0, 0))
    results = []
    for comp_id in range(3):
        backward = tuple((-value for value in UNITS[comp_id]))
        grad_term = stress_here - shifted_ext(lam_pad, *backward) * spread(backward)
        results.append(scale * (-laplace[comp_id] - grad_term))
    return jnp.stack(results)


def halo_x(array, depth):
    count = lax.axis_size("gx")
    width = array.shape[-3]
    reach = (depth + width - 1) // width
    lows, highs = [], []
    for dx in range(reach, 0, -1):
        need = min(width, depth - (dx - 1) * width)
        forward = [(i, i + dx) for i in range(count - dx)]
        backward = [(i + dx, i) for i in range(count - dx)]
        lows.append(lax.ppermute(array[..., width - need :, :, :], "gx", forward))
        highs.append(lax.ppermute(array[..., :need, :, :], "gx", backward))
    return jnp.concatenate(lows + [array] + highs[::-1], axis=-3)


def halo_x_split(array, depth_rhs, depth_coef):
    count = lax.axis_size("gx")
    width = array.shape[-3]
    reach = (depth_coef + width - 1) // width
    lows, highs = [], []
    for dx in range(reach, 0, -1):
        need = min(width, depth_coef - (dx - 1) * width)
        need_rhs = max(0, min(width, depth_rhs - (dx - 1) * width))
        forward = [(i, i + dx) for i in range(count - dx)]
        backward = [(i + dx, i) for i in range(count - dx)]
        if need_rhs == need:
            lows.append(lax.ppermute(array[..., width - need :, :, :], "gx", forward))
            highs.append(lax.ppermute(array[..., :need, :, :], "gx", backward))
            continue
        rest = need - need_rhs

        def pack(rhs_part, coef_part):
            flat = coef_part.reshape((-1, 1) + coef_part.shape[2:])
            return jnp.concatenate([rhs_part.reshape((-1, 1) + rhs_part.shape[2:]), flat], axis=0)

        def unpack(got, rhs_first):
            rhs_part = got[: 3 * need_rhs].reshape((3, need_rhs) + got.shape[2:])
            coef_part = got[3 * need_rhs :].reshape((2, need) + got.shape[2:])
            gap = jnp.zeros((3, rest) + got.shape[2:], got.dtype)
            rhs_full = jnp.concatenate([gap, rhs_part] if rhs_first else [rhs_part, gap], axis=1)
            return jnp.concatenate([rhs_full, coef_part], axis=0)

        got_low = lax.ppermute(
            pack(array[:3, width - need_rhs :], array[3:, width - need :]), "gx", forward
        )
        got_high = lax.ppermute(pack(array[:3, :need_rhs], array[3:, :need]), "gx", backward)
        lows.append(unpack(got_low, True))
        highs.append(unpack(got_high, False))
    return jnp.concatenate(lows + [array] + highs[::-1], axis=-3)


def halo_y(array, depth):
    count = lax.axis_size("gy")
    forward = [(i, i + 1) for i in range(count - 1)]
    backward = [(i + 1, i) for i in range(count - 1)]
    low = lax.ppermute(array[..., -depth:, :], "gy", forward)
    high = lax.ppermute(array[..., :depth, :], "gy", backward)
    return jnp.concatenate([low, array, high], axis=-2)


def inside_mask(width_x, width_y, depth_x, depth_y):
    gx = lax.axis_index("gx")
    gy = lax.axis_index("gy")
    total_x = width_x * lax.axis_size("gx")
    total_y = width_y * lax.axis_size("gy")
    xs = gx * width_x + jnp.arange(width_x + 2 * depth_x) - depth_x
    ys = gy * width_y + jnp.arange(width_y + 2 * depth_y) - depth_y
    ok_x = (xs >= 0) & (xs < total_x)
    ok_y = (ys >= 0) & (ys < total_y)
    return (ok_x[:, None] & ok_y[None, :])[:, :, None]


def smooth_ext(solution, residual, inverse_diag, mu, lam, steps):
    midpoint = 0.5 * (HIGH_BOUND + LOW_BOUND)
    halfwidth = 0.5 * (HIGH_BOUND - LOW_BOUND)
    sharpness = midpoint / halfwidth
    weight_old = 1.0 / sharpness

    def extent(array):
        return (
            (array.shape[-3] - solution.shape[-3]) // 2,
            (array.shape[-2] - solution.shape[-2]) // 2,
        )

    def fit(array, like):
        ax, ay = extent(array)
        bx, by = extent(like)
        return crop_xy(array, ax - bx, ay - by)

    direction = fit(inverse_diag, residual) * residual / midpoint
    solution = solution + fit(direction, solution)
    coef_like = jnp.zeros(residual.shape[-3:], residual.dtype)
    residual = crop(residual, 1) - apply_ext(direction, fit(mu, coef_like), fit(lam, coef_like), 1.0)
    for step_id in range(steps - 1):
        weight_new = 1.0 / (2.0 * sharpness - weight_old)
        direction = weight_new * weight_old * crop(direction, 1) + 2.0 * weight_new / halfwidth * (
            fit(inverse_diag, residual) * residual
        )
        solution = solution + fit(direction, solution)
        coef_like = jnp.zeros(residual.shape[-3:], residual.dtype)
        residual = crop(residual, 1) - apply_ext(
            direction, fit(mu, coef_like), fit(lam, coef_like), 1.0
        )
        weight_old = weight_new
    return (solution, residual)


def pair_matrix(coarse_z):
    fine = jnp.arange(2 * coarse_z) // 2
    return (fine[None, :] == jnp.arange(coarse_z)[:, None]).astype(jnp.float32)


def upsample_z(array, pairs):
    return jnp.einsum("...k,kj->...j", array, pairs, precision=lax.Precision.HIGHEST)


def restrict_z(array, pairs):
    return jnp.einsum("...j,kj->...k", array, pairs, precision=lax.Precision.HIGHEST)


def shards(rhs_field, shear_modulus, lame_lambda, group_start):
    width_x = rhs_field.shape[1]
    width_y = rhs_field.shape[2]
    width_z = rhs_field.shape[3]
    depth = SWEEPS
    gy = lax.axis_index("gy")
    count_y = lax.axis_size("gy")

    coarse_x = width_x // 2
    coarse_y = width_y // 2
    coarse_z = width_z // 2
    fine_reach = depth + 1
    res_rows = COARSE_SWEEPS + (depth + 2) // 2
    coef_rows = res_rows + 2
    deep_y = 2 * coef_rows

    stacked = jnp.concatenate([rhs_field, shear_modulus[None], lame_lambda[None]], axis=0)
    stacked = halo_x_split(stacked, depth, depth + 1)
    stacked = halo_y(stacked, deep_y)
    mu_ext = stacked[3]
    lam_ext = stacked[4]
    rhs_ext = crop(stacked[0:3], 1)
    inside = inside_mask(width_x, width_y, depth, deep_y - 1)
    inverse_diag = jnp.where(inside[None], 1.0 / diagonal_ext(mu_ext, lam_ext, 1.0), 0.0)

    solution, residual_deep = smooth_ext(
        jnp.zeros_like(rhs_field), rhs_ext, inverse_diag, mu_ext, lam_ext, SWEEPS
    )
    deep_r = (residual_deep.shape[2] - width_y) // 2
    residual_y = crop_xy(residual_deep, 0, deep_r - fine_reach)
    pairs = pair_matrix(coarse_z)
    res_win = restrict_z(crop_xy(residual_deep, 0, deep_r - 2 * res_rows), pairs)
    res_win = res_win.reshape(3, coarse_x, 2, coarse_y + 2 * res_rows, 2, coarse_z).sum(axis=(2, 4))
    fine_coef = crop_xy(jnp.stack([mu_ext, lam_ext]), depth + 1, deep_y - 2 * coef_rows)
    coef_win = restrict_z(fine_coef, pairs)
    coef_win = coef_win.reshape(2, coarse_x, 2, coarse_y + 2 * coef_rows, 2, coarse_z)
    coef_win = coef_win.sum(axis=(2, 4)) / 8.0
    coarse_res = res_win[:, :, res_rows : res_rows + coarse_y]
    starts = group_start[0]
    members = same_group(starts)
    cells_dev = coarse_x * coarse_y * coarse_z

    sums = coarse_res.sum(axis=(1, 2, 3))
    slots = jnp.where(jnp.arange(count_y)[:, None] == gy, sums[None, :], 0.0)
    all_sums = lax.psum(slots, "gy")

    def blocks(array, rows):
        gap = jnp.zeros(array.shape[:2] + (coarse_y - rows,) + array.shape[3:], array.dtype)
        low = jnp.concatenate([gap, array[:, :, :rows]], axis=2)
        own = array[:, :, rows : rows + coarse_y]
        high = jnp.concatenate([array[:, :, rows + coarse_y :], gap], axis=2)
        return jnp.stack([low, own, high], axis=1)

    window = jnp.concatenate([blocks(res_win, res_rows), blocks(coef_win, coef_rows)], axis=0)
    next_start = lax.dynamic_index_in_dim(starts, jnp.minimum(gy + 1, count_y - 1), 0, keepdims=False)
    own_start = lax.dynamic_index_in_dim(starts, gy, 0, keepdims=False)
    window_starts = jnp.stack([jnp.zeros_like(own_start), own_start, next_start])
    coef_pad = pad_groups(window[3:5], window_starts)
    coarse_diag = diagonal(coef_pad[0], coef_pad[1], 4.0)
    owners = gy - 1 + jnp.arange(3)
    valid = (owners >= 0) & (owners < count_y)
    usable = valid[None, :, None, None, None] & (coarse_diag > 0.0)
    coarse_inverse = jnp.where(usable, 1.0 / coarse_diag, 0.0)

    def coarse_apply(field):
        return operate(pad_groups(field, window_starts), coef_pad[0], coef_pad[1], 4.0)

    window_res = window[0:3]
    smoothed, coarse_left = smooth(
        jnp.zeros_like(window_res), window_res, coarse_inverse, coarse_apply, COARSE_SWEEPS
    )
    totals = jnp.sum(members[:, :, None] * all_sums[None, :, :], axis=1)
    group_cells = jnp.sum(members, axis=1) * cells_dev
    group_shift = totals / (SHIFT_SCALE * group_cells[:, None])
    window_shift = jnp.take(group_shift, jnp.clip(owners, 0, count_y - 1), axis=0)
    window_shift = jnp.where(valid[:, None], window_shift, 0.0)
    correction = smoothed + window_shift.T[:, :, None, None, None]
    correction = jnp.moveaxis(correction, 1, 2).reshape(3, coarse_x, 3 * coarse_y, coarse_z)
    reach_c = (depth + 2) // 2
    corr_y = correction[:, :, coarse_y - reach_c : 2 * coarse_y + reach_c, :]
    corr_z = upsample_z(corr_y, pairs)
    corr_rows = corr_z.shape[2]
    slab = 8 * ((corr_rows + 15) // 16)
    corr_pad = jnp.pad(corr_z, ((0, 0), (0, 0), (0, 2 * slab - corr_rows), (0, 0)))
    count_x = lax.axis_size("gx")
    edge_rows = residual_y.shape[2]
    lows_r, highs_r, lows_c, highs_c = [], [], [], []
    for dx in range(reach_c, 0, -1):
        forward = [(i, i + dx) for i in range(count_x - dx)]
        backward = [(i + dx, i) for i in range(count_x - dx)]
        need = min(width_x, depth - (dx - 1) * width_x)
        if need == width_x:
            corr_part = corr_pad.reshape(3, width_x, slab, width_z)
        else:
            corr_part = corr_pad
        send_low = jnp.concatenate([residual_y[:, width_x - need :], corr_part[:, : need]], axis=2)
        send_high = jnp.concatenate([residual_y[:, :need], corr_part[:, :need]], axis=2)
        got_low = lax.ppermute(send_low, "gx", forward)
        got_high = lax.ppermute(send_high, "gx", backward)
        lows_r.append(got_low[:, :, :edge_rows])
        highs_r.append(got_high[:, :, :edge_rows])
        lows_c.append(got_low[:, :, edge_rows:].reshape(3, 1, -1, width_z)[:, :, :corr_rows])
        highs_c.append(got_high[:, :, edge_rows:].reshape(3, 1, -1, width_z)[:, :, :corr_rows])
    residual_ext = crop_xy(jnp.concatenate(lows_r + [residual_y] + highs_r[::-1], axis=1), 0, 1)
    corr_cols = jnp.concatenate(lows_c + [corr_z] + highs_c[::-1], axis=1)
    fine_corr = jnp.broadcast_to(
        corr_cols[:, :, None, :, None, :],
        (3, corr_cols.shape[1], 2, corr_rows, 2, width_z),
    ).reshape(3, 2 * corr_cols.shape[1], 2 * corr_rows, width_z)
    fine_depth = 2 * reach_c
    fine_corr = crop(fine_corr, fine_depth - fine_reach)
    solution = solution + crop(fine_corr, fine_reach)
    coef_cut = (mu_ext.shape[-2] - fine_corr.shape[-2]) // 2
    residual_ext = residual_ext - apply_ext(
        fine_corr, crop_xy(mu_ext, 0, coef_cut), crop_xy(lam_ext, 0, coef_cut), 1.0
    )
    solution, residual = smooth_ext(
        solution, residual_ext, inverse_diag, mu_ext, lam_ext, SWEEPS
    )
    return (solution, residual)


def solution(mesh):
    return jax.shard_map(
        shards,
        mesh=mesh,
        in_specs=(
            P(None, "gx", "gy", None),
            P("gx", "gy", None),
            P("gx", "gy", None),
            P("gx", None),
        ),
        out_specs=(P(None, "gx", "gy", None), P(None, "gx", "gy", None)),
        check_vma=False,
    )
```

```python
import jax
import jax.numpy as jnp
from jax import lax
from jax.sharding import PartitionSpec as P

SWEEPS = 3
COARSE_SWEEPS = 4


LOW_BOUND = 0.5
HIGH_BOUND = 6.0
SHIFT_SCALE = 48.0
UNITS = ((1, 0, 0), (0, 1, 0), (0, 0, 1))


def shifted(array, step_x, step_y, step_z):
    size_x = array.shape[-3] - 2
    size_y = array.shape[-2] - 2
    size_z = array.shape[-1] - 2
    return array[
        ...,
        1 + step_x : 1 + step_x + size_x,
        1 + step_y : 1 + step_y + size_y,
        1 + step_z : 1 + step_z + size_z,
    ]


def diagonal(mu_pad, lam_pad, scale):
    mu_centre = shifted(mu_pad, 0, 0, 0)
    lam_centre = shifted(lam_pad, 0, 0, 0)
    faces = 0.0
    for unit in UNITS:
        backward = tuple((-value for value in unit))
        faces = (
            faces
            + 0.5 * (mu_centre + shifted(mu_pad, *unit))
            + 0.5 * (mu_centre + shifted(mu_pad, *backward))
        )
    results = []
    for unit in UNITS:
        backward = tuple((-value for value in unit))
        results.append(scale * (faces + lam_centre + shifted(lam_pad, *backward)))
    return jnp.stack(results)


def operate(field_pad, mu_pad, lam_pad, scale):
    mu_centre = shifted(mu_pad, 0, 0, 0)
    lam_centre = shifted(lam_pad, 0, 0, 0)
    components = [field_pad[0], field_pad[1], field_pad[2]]
    centres = [shifted(value, 0, 0, 0) for value in components]
    laplace = [0.0, 0.0, 0.0]
    for unit in UNITS:
        backward = tuple((-value for value in unit))
        face_up = 0.5 * (mu_centre + shifted(mu_pad, *unit))
        face_down = 0.5 * (mu_centre + shifted(mu_pad, *backward))
        for comp_id in range(3):
            laplace[comp_id] = (
                laplace[comp_id]
                + face_up * (shifted(components[comp_id], *unit) - centres[comp_id])
                - face_down * (centres[comp_id] - shifted(components[comp_id], *backward))
            )

    def spread(offset):
        total = 0.0
        for comp_id in range(3):
            ahead = tuple((offset[axis_id] + UNITS[comp_id][axis_id] for axis_id in range(3)))
            total = total + (
                shifted(components[comp_id], *ahead) - shifted(components[comp_id], *offset)
            )
        return total

    stress_here = lam_centre * spread((0, 0, 0))
    results = []
    for comp_id in range(3):
        backward = tuple((-value for value in UNITS[comp_id]))
        grad_term = stress_here - shifted(lam_pad, *backward) * spread(backward)
        results.append(scale * (-laplace[comp_id] - grad_term))
    return jnp.stack(results)


def smooth(solution, residual, inverse_diag, apply_fn, steps):
    midpoint = 0.5 * (HIGH_BOUND + LOW_BOUND)
    halfwidth = 0.5 * (HIGH_BOUND - LOW_BOUND)
    sharpness = midpoint / halfwidth
    weight_old = 1.0 / sharpness
    direction = inverse_diag * residual / midpoint
    solution = solution + direction
    residual = residual - apply_fn(direction)
    for step_id in range(steps - 1):
        weight_new = 1.0 / (2.0 * sharpness - weight_old)
        direction = weight_new * weight_old * direction + 2.0 * weight_new / halfwidth * (
            inverse_diag * residual
        )
        solution = solution + direction
        residual = residual - apply_fn(direction)
        weight_old = weight_new
    return (solution, residual)


def pad_groups(array, starts):
    cont = jnp.where(starts[..., 1:] == 0, 1.0, 0.0)
    closed = jnp.zeros_like(cont[..., :1])
    lower = jnp.concatenate([closed, cont], axis=-1)[..., None, None, None]
    upper = jnp.concatenate([cont, closed], axis=-1)[..., None, None, None]
    below = (
        jnp.concatenate(
            [jnp.zeros_like(array[..., :1, :, :1, :]), array[..., :-1, :, -1:, :]], axis=-4
        )
        * lower
    )
    above = (
        jnp.concatenate(
            [array[..., 1:, :, :1, :], jnp.zeros_like(array[..., :1, :, :1, :])], axis=-4
        )
        * upper
    )
    joined = jnp.concatenate([below, array, above], axis=-2)
    widths = [(0, 0)] * (joined.ndim - 3) + [(1, 1), (0, 0), (1, 1)]
    return jnp.pad(joined, widths)


def same_group(starts):
    count = starts.shape[-1]
    marks = jnp.where(jnp.arange(count, dtype=jnp.int32) > 0, starts, 0)
    labels = jnp.cumsum(marks, axis=-1)
    return jnp.where(labels[..., :, None] == labels[..., None, :], 1.0, 0.0).astype(jnp.float32)


def crop_xy(array, cut_x, cut_y):
    size_x = array.shape[-3]
    size_y = array.shape[-2]
    return array[..., cut_x : size_x - cut_x, cut_y : size_y - cut_y, :]


def crop(array, cut):
    if cut == 0:
        return array
    return array[..., cut:-cut, cut:-cut, :]


def shifted_ext(array, step_x, step_y, step_z):
    size_x = array.shape[-3] - 2
    size_y = array.shape[-2] - 2
    inner = array[..., 1 + step_x : 1 + step_x + size_x, 1 + step_y : 1 + step_y + size_y, :]
    if step_z == 0:
        return inner
    zero = jnp.zeros_like(inner[..., :1])
    if step_z > 0:
        return jnp.concatenate([inner[..., 1:], zero], axis=-1)
    return jnp.concatenate([zero, inner[..., :-1]], axis=-1)


def diagonal_ext(mu_pad, lam_pad, scale):
    mu_centre = shifted_ext(mu_pad, 0, 0, 0)
    lam_centre = shifted_ext(lam_pad, 0, 0, 0)
    faces = 0.0
    for unit in UNITS:
        backward = tuple((-value for value in unit))
        faces = (
            faces
            + 0.5 * (mu_centre + shifted_ext(mu_pad, *unit))
            + 0.5 * (mu_centre + shifted_ext(mu_pad, *backward))
        )
    results = []
    for unit in UNITS:
        backward = tuple((-value for value in unit))
        results.append(scale * (faces + lam_centre + shifted_ext(lam_pad, *backward)))
    return jnp.stack(results)


def apply_ext(field_pad, mu_pad, lam_pad, scale):
    mu_centre = shifted_ext(mu_pad, 0, 0, 0)
    lam_centre = shifted_ext(lam_pad, 0, 0, 0)
    components = [field_pad[0], field_pad[1], field_pad[2]]
    centres = [shifted_ext(value, 0, 0, 0) for value in components]
    laplace = [0.0, 0.0, 0.0]
    for unit in UNITS:
        backward = tuple((-value for value in unit))
        face_up = 0.5 * (mu_centre + shifted_ext(mu_pad, *unit))
        face_down = 0.5 * (mu_centre + shifted_ext(mu_pad, *backward))
        for comp_id in range(3):
            laplace[comp_id] = (
                laplace[comp_id]
                + face_up * (shifted_ext(components[comp_id], *unit) - centres[comp_id])
                - face_down * (centres[comp_id] - shifted_ext(components[comp_id], *backward))
            )

    def spread(offset):
        total = 0.0
        for comp_id in range(3):
            ahead = tuple((offset[axis_id] + UNITS[comp_id][axis_id] for axis_id in range(3)))
            total = total + (
                shifted_ext(components[comp_id], *ahead)
                - shifted_ext(components[comp_id], *offset)
            )
        return total

    stress_here = lam_centre * spread((0, 0, 0))
    results = []
    for comp_id in range(3):
        backward = tuple((-value for value in UNITS[comp_id]))
        grad_term = stress_here - shifted_ext(lam_pad, *backward) * spread(backward)
        results.append(scale * (-laplace[comp_id] - grad_term))
    return jnp.stack(results)


def halo_x(array, depth):
    count = lax.axis_size("gx")
    width = array.shape[-3]
    reach = (depth + width - 1) // width
    lows, highs = [], []
    for dx in range(reach, 0, -1):
        need = min(width, depth - (dx - 1) * width)
        forward = [(i, i + dx) for i in range(count - dx)]
        backward = [(i + dx, i) for i in range(count - dx)]
        lows.append(lax.ppermute(array[..., width - need :, :, :], "gx", forward))
        highs.append(lax.ppermute(array[..., :need, :, :], "gx", backward))
    return jnp.concatenate(lows + [array] + highs[::-1], axis=-3)


def halo_y(array, depth):
    count = lax.axis_size("gy")
    forward = [(i, i + 1) for i in range(count - 1)]
    backward = [(i + 1, i) for i in range(count - 1)]
    low = lax.ppermute(array[..., -depth:, :], "gy", forward)
    high = lax.ppermute(array[..., :depth, :], "gy", backward)
    return jnp.concatenate([low, array, high], axis=-2)


def inside_mask(width_x, width_y, depth_x, depth_y):
    gx = lax.axis_index("gx")
    gy = lax.axis_index("gy")
    total_x = width_x * lax.axis_size("gx")
    total_y = width_y * lax.axis_size("gy")
    xs = gx * width_x + jnp.arange(width_x + 2 * depth_x) - depth_x
    ys = gy * width_y + jnp.arange(width_y + 2 * depth_y) - depth_y
    ok_x = (xs >= 0) & (xs < total_x)
    ok_y = (ys >= 0) & (ys < total_y)
    return (ok_x[:, None] & ok_y[None, :])[:, :, None]


def smooth_ext(solution, residual, inverse_diag, mu, lam, steps):
    midpoint = 0.5 * (HIGH_BOUND + LOW_BOUND)
    halfwidth = 0.5 * (HIGH_BOUND - LOW_BOUND)
    sharpness = midpoint / halfwidth
    weight_old = 1.0 / sharpness

    def extent(array):
        return (
            (array.shape[-3] - solution.shape[-3]) // 2,
            (array.shape[-2] - solution.shape[-2]) // 2,
        )

    def fit(array, like):
        ax, ay = extent(array)
        bx, by = extent(like)
        return crop_xy(array, ax - bx, ay - by)

    direction = fit(inverse_diag, residual) * residual / midpoint
    solution = solution + fit(direction, solution)
    coef_like = jnp.zeros(residual.shape[-3:], residual.dtype)
    residual = crop(residual, 1) - apply_ext(direction, fit(mu, coef_like), fit(lam, coef_like), 1.0)
    for step_id in range(steps - 1):
        weight_new = 1.0 / (2.0 * sharpness - weight_old)
        direction = weight_new * weight_old * crop(direction, 1) + 2.0 * weight_new / halfwidth * (
            fit(inverse_diag, residual) * residual
        )
        solution = solution + fit(direction, solution)
        coef_like = jnp.zeros(residual.shape[-3:], residual.dtype)
        residual = crop(residual, 1) - apply_ext(
            direction, fit(mu, coef_like), fit(lam, coef_like), 1.0
        )
        weight_old = weight_new
    return (solution, residual)


def pair_matrix(coarse_z):
    fine = jnp.arange(2 * coarse_z) // 2
    return (fine[None, :] == jnp.arange(coarse_z)[:, None]).astype(jnp.float32)


def upsample_z(array, pairs):
    return jnp.einsum("...k,kj->...j", array, pairs, precision=lax.Precision.HIGHEST)


def restrict_z(array, pairs):
    return jnp.einsum("...j,kj->...k", array, pairs, precision=lax.Precision.HIGHEST)


def shards(rhs_field, shear_modulus, lame_lambda, group_start):
    width_x = rhs_field.shape[1]
    width_y = rhs_field.shape[2]
    width_z = rhs_field.shape[3]
    depth = SWEEPS
    gy = lax.axis_index("gy")
    count_y = lax.axis_size("gy")

    coarse_x = width_x // 2
    coarse_y = width_y // 2
    coarse_z = width_z // 2
    fine_reach = depth + 1
    res_rows = COARSE_SWEEPS + (depth + 2) // 2
    coef_rows = res_rows + 2
    deep_y = 2 * coef_rows

    stacked = jnp.concatenate([rhs_field, shear_modulus[None], lame_lambda[None]], axis=0)
    stacked = halo_x(stacked, depth + 1)
    coef_x = stacked[3:5]
    rhs_x = stacked[0:3, 1:-1]
    count_y = lax.axis_size("gy")

    def rows_of(part, pick):
        return part[..., pick, :].reshape((-1,) + part[..., pick, :].shape[-2:])

    low_rows = slice(width_y - deep_y, width_y)
    high_rows = slice(0, deep_y)
    send_low = jnp.concatenate([rows_of(coef_x, low_rows), rows_of(rhs_x, low_rows)], axis=0)
    send_high = jnp.concatenate([rows_of(coef_x, high_rows), rows_of(rhs_x, high_rows)], axis=0)
    got_low = lax.ppermute(send_low, "gy", [(i, i + 1) for i in range(count_y - 1)])
    got_high = lax.ppermute(send_high, "gy", [(i + 1, i) for i in range(count_y - 1)])
    split = coef_x.shape[0] * coef_x.shape[1]
    coef_shape = coef_x.shape[:2] + (deep_y, width_z)
    rhs_shape = rhs_x.shape[:2] + (deep_y, width_z)
    coef_ext = jnp.concatenate(
        [got_low[:split].reshape(coef_shape), coef_x, got_high[:split].reshape(coef_shape)], axis=2
    )
    rhs_full = jnp.concatenate(
        [got_low[split:].reshape(rhs_shape), rhs_x, got_high[split:].reshape(rhs_shape)], axis=2
    )
    mu_ext = coef_ext[0]
    lam_ext = coef_ext[1]
    rhs_ext = rhs_full[:, :, 1:-1]
    inside = inside_mask(width_x, width_y, depth, deep_y - 1)
    inverse_diag = jnp.where(inside[None], 1.0 / diagonal_ext(mu_ext, lam_ext, 1.0), 0.0)

    solution, residual_deep = smooth_ext(
        jnp.zeros_like(rhs_field), rhs_ext, inverse_diag, mu_ext, lam_ext, SWEEPS
    )
    deep_r = (residual_deep.shape[2] - width_y) // 2
    residual_y = crop_xy(residual_deep, 0, deep_r - fine_reach)
    pairs = pair_matrix(coarse_z)
    res_win = restrict_z(crop_xy(residual_deep, 0, deep_r - 2 * res_rows), pairs)
    res_win = res_win.reshape(3, coarse_x, 2, coarse_y + 2 * res_rows, 2, coarse_z).sum(axis=(2, 4))
    fine_coef = crop_xy(jnp.stack([mu_ext, lam_ext]), depth + 1, deep_y - 2 * coef_rows)
    coef_win = restrict_z(fine_coef, pairs)
    coef_win = coef_win.reshape(2, coarse_x, 2, coarse_y + 2 * coef_rows, 2, coarse_z)
    coef_win = coef_win.sum(axis=(2, 4)) / 8.0
    coarse_res = res_win[:, :, res_rows : res_rows + coarse_y]
    starts = group_start[0]
    members = same_group(starts)
    cells_dev = coarse_x * coarse_y * coarse_z

    sums = coarse_res.sum(axis=(1, 2, 3))
    slots = jnp.where(jnp.arange(count_y)[:, None] == gy, sums[None, :], 0.0)
    all_sums = lax.psum(slots, "gy")

    def blocks(array, rows):
        gap = jnp.zeros(array.shape[:2] + (coarse_y - rows,) + array.shape[3:], array.dtype)
        low = jnp.concatenate([gap, array[:, :, :rows]], axis=2)
        own = array[:, :, rows : rows + coarse_y]
        high = jnp.concatenate([array[:, :, rows + coarse_y :], gap], axis=2)
        return jnp.stack([low, own, high], axis=1)

    window = jnp.concatenate([blocks(res_win, res_rows), blocks(coef_win, coef_rows)], axis=0)
    next_start = lax.dynamic_index_in_dim(starts, jnp.minimum(gy + 1, count_y - 1), 0, keepdims=False)
    own_start = lax.dynamic_index_in_dim(starts, gy, 0, keepdims=False)
    window_starts = jnp.stack([jnp.zeros_like(own_start), own_start, next_start])
    coef_pad = pad_groups(window[3:5], window_starts)
    coarse_diag = diagonal(coef_pad[0], coef_pad[1], 4.0)
    owners = gy - 1 + jnp.arange(3)
    valid = (owners >= 0) & (owners < count_y)
    usable = valid[None, :, None, None, None] & (coarse_diag > 0.0)
    coarse_inverse = jnp.where(usable, 1.0 / coarse_diag, 0.0)

    def coarse_apply(field):
        return operate(pad_groups(field, window_starts), coef_pad[0], coef_pad[1], 4.0)

    window_res = window[0:3]
    smoothed, coarse_left = smooth(
        jnp.zeros_like(window_res), window_res, coarse_inverse, coarse_apply, COARSE_SWEEPS
    )
    totals = jnp.sum(members[:, :, None] * all_sums[None, :, :], axis=1)
    group_cells = jnp.sum(members, axis=1) * cells_dev
    group_shift = totals / (SHIFT_SCALE * group_cells[:, None])
    window_shift = jnp.take(group_shift, jnp.clip(owners, 0, count_y - 1), axis=0)
    window_shift = jnp.where(valid[:, None], window_shift, 0.0)
    correction = smoothed + window_shift.T[:, :, None, None, None]
    correction = jnp.moveaxis(correction, 1, 2).reshape(3, coarse_x, 3 * coarse_y, coarse_z)
    reach_c = (depth + 2) // 2
    corr_y = correction[:, :, coarse_y - reach_c : 2 * coarse_y + reach_c, :]
    corr_z = upsample_z(corr_y, pairs)
    corr_rows = corr_z.shape[2]
    slab = 8 * ((corr_rows + 15) // 16)
    corr_pad = jnp.pad(corr_z, ((0, 0), (0, 0), (0, 2 * slab - corr_rows), (0, 0)))
    count_x = lax.axis_size("gx")
    edge_rows = residual_y.shape[2]
    lows_r, highs_r, lows_c, highs_c = [], [], [], []
    for dx in range(reach_c, 0, -1):
        forward = [(i, i + dx) for i in range(count_x - dx)]
        backward = [(i + dx, i) for i in range(count_x - dx)]
        need = min(width_x, depth - (dx - 1) * width_x)
        if need == width_x:
            corr_part = corr_pad.reshape(3, width_x, slab, width_z)
        else:
            corr_part = corr_pad
        send_low = jnp.concatenate([residual_y[:, width_x - need :], corr_part[:, : need]], axis=2)
        send_high = jnp.concatenate([residual_y[:, :need], corr_part[:, :need]], axis=2)
        got_low = lax.ppermute(send_low, "gx", forward)
        got_high = lax.ppermute(send_high, "gx", backward)
        lows_r.append(got_low[:, :, :edge_rows])
        highs_r.append(got_high[:, :, :edge_rows])
        lows_c.append(got_low[:, :, edge_rows:].reshape(3, 1, -1, width_z)[:, :, :corr_rows])
        highs_c.append(got_high[:, :, edge_rows:].reshape(3, 1, -1, width_z)[:, :, :corr_rows])
    residual_ext = crop_xy(jnp.concatenate(lows_r + [residual_y] + highs_r[::-1], axis=1), 0, 1)
    corr_cols = jnp.concatenate(lows_c + [corr_z] + highs_c[::-1], axis=1)
    fine_corr = jnp.broadcast_to(
        corr_cols[:, :, None, :, None, :],
        (3, corr_cols.shape[1], 2, corr_rows, 2, width_z),
    ).reshape(3, 2 * corr_cols.shape[1], 2 * corr_rows, width_z)
    fine_depth = 2 * reach_c
    fine_corr = crop(fine_corr, fine_depth - fine_reach)
    solution = solution + crop(fine_corr, fine_reach)
    coef_cut = (mu_ext.shape[-2] - fine_corr.shape[-2]) // 2
    residual_ext = residual_ext - apply_ext(
        fine_corr, crop_xy(mu_ext, 0, coef_cut), crop_xy(lam_ext, 0, coef_cut), 1.0
    )
    solution, residual = smooth_ext(
        solution, residual_ext, inverse_diag, mu_ext, lam_ext, SWEEPS
    )
    return (solution, residual)


def solution(mesh):
    return jax.shard_map(
        shards,
        mesh=mesh,
        in_specs=(
            P(None, "gx", "gy", None),
            P("gx", "gy", None),
            P("gx", "gy", None),
            P("gx", None),
        ),
        out_specs=(P(None, "gx", "gy", None), P(None, "gx", "gy", None)),
        check_vma=False,
    )
```
